256 devices in a mesh: tm: 8 (over x, core), space: 32 (over y, z).
Axes of the slice: x: 4, y: 4, z: 8, core: 2. Of those that a mesh axis runs over, the one named last changes fastest.
Arguments:
- snapshots: bfloat16 [2016, 5, 64, 8, 128], P('tm', None, 'space'), may hold values from -6 to 6
- picks: int32 [1792], P('tm'), may hold values from 0 to 251, as said below
- basis: bfloat16 [32, 5, 64, 8, 128], P(None, None, 'space'), may hold values from -0.01953125 to 0.01953125
- kappa: float32 [5, 64, 8, 128], P(None, 'space'), may hold values from 0.03 to 0.16
Outputs:
- coefficients: float32 [1792, 32], P('tm')
- factor: float32 [561, 561], replicated
The draws below stay inside these ranges and needn't reach their ends.
Inputs may be any that keep to these rules, and one draw needn't show every extreme that they name: `picks`: within each time group's 224 consecutive entries the indices are distinct, and 0 and 251 both occur.
All inputs are finite; a program needn't handle non-finite values.
Results may differ from the reference program's by a relative error of at most 0.0003.
Values may be sent and summed in bfloat16 or wider, within the bound.
No kernel may reach another device: no remote copies, remote signals or barrier semaphores. Data moves between devices by JAX's collectives and lax.ppermute only.
A program may use at most 64 MiB of HBM per device.

```python
import math
import jax
import jax.numpy as jnp
import numpy as np
from jax import lax

MODES = 32
VARS = 5
NY = 8
NZ = 128
PICKS = 224
STORED = 252
TIME = 1792
NX = 64
N_TM = 8


def draw_picks(key, part):
    groups = TIME // PICKS

    def one_group(group_key):
        first_key, second_key = jax.random.split(group_key)
        inner = jax.random.permutation(first_key, STORED - 2)[:PICKS - 2] + 1
        ends = jnp.array([0, STORED - 1], dtype=jnp.int32)
        row = jnp.concatenate([ends, inner.astype(jnp.int32)])
        return jax.random.permutation(second_key, row)
    keys = jax.random.split(jax.random.fold_in(key, 7), groups)
    return jax.vmap(one_group)(keys).reshape(-1).astype(jnp.int32)


def shard_levels(own_key, extent, cuts, low, largest):
    factor_of = 1.0
    for position, parts in cuts:
        heights = jax.random.uniform(jax.random.fold_in(jax.random.fold_in(own_key, 6), position), (parts,), jnp.float32, low / len(cuts), largest / len(cuts))
        factor_of = factor_of * jnp.repeat(jnp.exp(heights), extent[position] // parts).reshape((-1,) + (1,) * (len(extent) - 1 - position))
    return factor_of


def bell_draw(stream_key, extent, scale, limit, cuts=(), kind=jnp.bfloat16):
    values = jax.random.normal(stream_key, extent, jnp.float32) * scale
    if len(cuts) > 0:
        values = shard_levels(stream_key, extent, cuts, -0.22, 0.18) * values
    return jnp.clip(values, min=-limit, max=limit).astype(kind)


def setup_inputs(seed: int = 0) -> dict:
    streams_of = jax.random.split(jax.random.key(seed), 5)
    snapshots = bell_draw(streams_of[0], (STORED * N_TM, VARS, NX, NY, NZ), 1.0, 6.0, ((0, 8), (2, 32)))
    picks = draw_picks(jax.random.fold_in(streams_of[4], 71), 0)
    basis = bell_draw(streams_of[2], (MODES, VARS, NX, NY, NZ), (VARS * NX * NY * NZ // 4) ** -0.5, 0.01953125, ((2, 32),))
    kappa = jnp.clip(jnp.exp(math.log(0.16) - 1.6739764 * jax.random.uniform(streams_of[3], (VARS, NX, NY, NZ), jnp.float32) ** shard_levels(streams_of[3], (VARS, NX, NY, NZ), ((1, 32),), -0.2, 0.2)), 0.03, 0.16)
    return {"snapshots": snapshots, "picks": picks, "basis": basis, "kappa": kappa}


def smooth(field, kappa):
    padded = jnp.pad(field, ((0, 0), (1, 1), (1, 1), (1, 1)))
    beside = padded[:, 2:, 1:-1, 1:-1] + padded[:, :-2, 1:-1, 1:-1]
    beside = beside + padded[:, 1:-1, 2:, 1:-1] + padded[:, 1:-1, :-2, 1:-1]
    beside = beside + padded[:, 1:-1, 1:-1, 2:] + padded[:, 1:-1, 1:-1, :-2]
    return field + kappa * (beside - 6.0 * field)

def expand(coeffs):
    count = coeffs.shape[1]
    first, second = np.triu_indices(count)
    quad = coeffs[:, first] * coeffs[:, second]
    ones = jnp.ones((coeffs.shape[0], 1), coeffs.dtype)
    return jnp.concatenate([ones, coeffs, quad], axis=1)

def reference(snapshots, picks, basis, kappa):
    basis_flat = basis.astype(jnp.float32).reshape(basis.shape[0], -1)
    steps_all = jnp.arange(TIME, dtype=jnp.int32)

    def one_row(pair):
        step, pick = pair
        source = (step // PICKS * STORED + pick).astype(jnp.int32)
        taken = lax.dynamic_index_in_dim(snapshots, source, 0, keepdims=False)
        filtered = smooth(taken.astype(jnp.float32), kappa)
        flat = filtered.reshape(-1)
        return jnp.dot(basis_flat, flat, precision=lax.Precision.HIGHEST)
    coefficients = lax.map(one_row, (steps_all, picks))
    features = expand(coefficients)
    gram = jnp.dot(features.T, features, precision=lax.Precision.HIGHEST) / TIME
    factor = jnp.linalg.cholesky(gram).T
    return (coefficients, factor)
```

```python
import jax
import jax.numpy as jnp
import numpy as np
from jax import lax
from jax.sharding import PartitionSpec as P


def neighbour_planes(block, axis, dim):
    count = lax.axis_size(axis)
    forward = [(i, i + 1) for i in range(count - 1)]
    backward = [(target, source) for source, target in forward]
    width = block.shape[dim]
    low = lax.ppermute(lax.slice_in_dim(block, width - 1, width, axis=dim), axis, forward)
    high = lax.ppermute(lax.slice_in_dim(block, 0, 1, axis=dim), axis, backward)
    return jnp.concatenate([low, block, high], axis=dim)


def adjoint_basis(basis, kappa):
    wide = basis.astype(jnp.float32)
    scaled = kappa[None] * wide
    padded = neighbour_planes(scaled, "space", 2)
    padded = jnp.pad(padded, ((0, 0), (0, 0), (0, 0), (1, 1), (1, 1)))
    center = padded[:, :, 1:-1, 1:-1, 1:-1]
    beside = padded[:, :, 2:, 1:-1, 1:-1] + padded[:, :, :-2, 1:-1, 1:-1]
    beside = beside + padded[:, :, 1:-1, 2:, 1:-1] + padded[:, :, 1:-1, :-2, 1:-1]
    beside = beside + padded[:, :, 1:-1, 1:-1, 2:] + padded[:, :, 1:-1, 1:-1, :-2]
    return wide + (beside - 6.0 * center)


def butterfly_sum(x, axis):
    count = lax.axis_size(axis)
    if count & (count - 1):
        return lax.psum(x, axis)
    step = 1
    while step < count:
        x = x + lax.ppermute(x, axis, [(i, i ^ step) for i in range(count)])
        step *= 2
    return x


def butterfly_gather(x, axis, dim):
    count = lax.axis_size(axis)
    if count & (count - 1):
        return lax.all_gather(x, axis, axis=dim, tiled=True)
    index = lax.axis_index(axis)
    step = 1
    while step < count:
        other = lax.ppermute(x, axis, [(i, i ^ step) for i in range(count)])
        low = (index // step) % 2 == 0
        x = jnp.where(low, jnp.concatenate([x, other], dim), jnp.concatenate([other, x], dim))
        step *= 2
    return x


def expand_rows(coeffs_t):
    count = coeffs_t.shape[0]
    first, second = np.triu_indices(count)
    quad = jnp.take(coeffs_t, first, axis=0) * jnp.take(coeffs_t, second, axis=0)
    ones = jnp.ones((1, coeffs_t.shape[1]), coeffs_t.dtype)
    return jnp.concatenate([ones, coeffs_t, quad], axis=0)


def body(snapshots, picks, basis, kappa):
    modes = basis.shape[0]
    adjoint = adjoint_basis(basis, kappa).reshape(modes, -1)
    stored = snapshots.shape[0]
    flat = snapshots.reshape(stored, -1).astype(jnp.float32)
    partial_t = lax.dot_general(
        adjoint,
        flat,
        (((1,), (1,)), ((), ())),
        precision=lax.Precision.HIGHEST,
        preferred_element_type=jnp.float32,
    )
    part_t = jnp.take(partial_t, picks, axis=1)
    own_t = butterfly_sum(part_t, "space")
    coeffs_t = butterfly_gather(own_t, "tm", 1)
    features_t = expand_rows(coeffs_t)
    gram = lax.dot_general(
        features_t,
        features_t,
        (((1,), (1,)), ((), ())),
        precision=lax.Precision.HIGHEST,
        preferred_element_type=jnp.float32,
    ) / coeffs_t.shape[1]
    factor = jnp.linalg.cholesky(gram).T
    return (own_t.T, factor)


def solution(mesh):
    in_specs = (
        P("tm", None, "space", None, None),
        P("tm"),
        P(None, None, "space", None, None),
        P(None, "space", None, None),
    )
    out_specs = (P("tm", None), P())
    return jax.shard_map(body, mesh=mesh, in_specs=in_specs, out_specs=out_specs, check_vma=False)
```

```python
import functools

import jax
import jax.numpy as jnp
import numpy as np
from jax import lax
from jax.experimental import pallas as pl
from jax.experimental.pallas import tpu as pltpu
from jax.sharding import PartitionSpec as P

PANEL = 128


def split3(x):
    hi = x.astype(jnp.bfloat16)
    rest = x - hi.astype(jnp.float32)
    mid = rest.astype(jnp.bfloat16)
    lo = (rest - mid.astype(jnp.float32)).astype(jnp.bfloat16)
    return hi, mid, lo


def dot3(a, b):
    a1, a2, a3 = split3(a)
    b1, b2, b3 = split3(b)
    def d(x, y):
        return jnp.dot(x, y, preferred_element_type=jnp.float32)
    return d(a1, b1) + (d(a1, b2) + d(a2, b1)) + (d(a1, b3) + d(a3, b1) + d(a2, b2))


def chol_kernel(a_ref, r_ref, w_ref, blk_ref, *, size, valid):
    panels = size // PANEL
    r_ref[...] = jnp.zeros((size, size), jnp.float32)
    w_ref[...] = a_ref[...]
    rows = lax.broadcasted_iota(jnp.int32, (PANEL, 2 * PANEL), 0)
    lanes = lax.broadcasted_iota(jnp.int32, (PANEL, 2 * PANEL), 1)
    eye = (rows[:, :PANEL] == lanes[:, :PANEL]).astype(jnp.float32)
    row_lanes = lax.broadcasted_iota(jnp.int32, (1, 2 * PANEL), 1)
    col_rows = lax.broadcasted_iota(jnp.int32, (PANEL, 1), 0)
    for p in range(panels):
        c0 = p * PANEL
        c1 = c0 + PANEL
        steps = min(PANEL, valid - c0)
        blk_ref[:, :PANEL] = w_ref[c0:c1, c0:c1]
        blk_ref[:, PANEL:] = eye

        def step(j, carry):
            row = blk_ref[pl.ds(j, 1), :]
            pivot = jnp.sum(jnp.where(row_lanes == j, row, 0.0), axis=1, keepdims=True)
            scale = lax.rsqrt(pivot)
            scaled = row * scale
            block = blk_ref[...]
            column = jnp.sum(jnp.where(lanes[:, :PANEL] == j, block[:, :PANEL], 0.0), axis=1, keepdims=True)
            coef = jnp.where(col_rows > j, column * scale, 0.0)
            updated = block - coef * scaled
            blk_ref[...] = jnp.where(rows == j, scaled, updated)
            return carry

        lax.fori_loop(0, steps, step, 0)
        block = blk_ref[...]
        upper = jnp.where(lanes[:, :PANEL] >= rows[:, :PANEL], block[:, :PANEL], 0.0)
        r_ref[c0:c1, c0:c1] = upper
        if p + 1 < panels:
            inv_t = block[:, PANEL:]
            right = dot3(inv_t, w_ref[c0:c1, c1:size])
            r_ref[c0:c1, c1:size] = right
            w_ref[c1:size, c1:size] = w_ref[c1:size, c1:size] - dot3(right.T, right)


def cholesky_upper(gram):
    n = gram.shape[0]
    size = -(-n // PANEL) * PANEL
    padded = jnp.pad(gram, ((0, size - n), (0, size - n)))
    fill = (jnp.arange(size) >= n).astype(jnp.float32)
    padded = padded + jnp.diag(fill)
    out = pl.pallas_call(
        functools.partial(chol_kernel, size=size, valid=n),
        out_shape=jax.ShapeDtypeStruct((size, size), jnp.float32),
        scratch_shapes=[pltpu.VMEM((size, size), jnp.float32), pltpu.VMEM((PANEL, 2 * PANEL), jnp.float32)],
    )(padded)
    return out[:n, :n]


def neighbour_planes(block, axis, dim):
    count = lax.axis_size(axis)
    forward = [(i, i + 1) for i in range(count - 1)]
    backward = [(target, source) for source, target in forward]
    width = block.shape[dim]
    low = lax.ppermute(lax.slice_in_dim(block, width - 1, width, axis=dim), axis, forward)
    high = lax.ppermute(lax.slice_in_dim(block, 0, 1, axis=dim), axis, backward)
    return jnp.concatenate([low, block, high], axis=dim)


def adjoint_basis(basis, kappa):
    wide = basis.astype(jnp.float32)
    scaled = kappa[None] * wide
    padded = neighbour_planes(scaled, "space", 2)
    padded = jnp.pad(padded, ((0, 0), (0, 0), (0, 0), (1, 1), (1, 1)))
    center = padded[:, :, 1:-1, 1:-1, 1:-1]
    beside = padded[:, :, 2:, 1:-1, 1:-1] + padded[:, :, :-2, 1:-1, 1:-1]
    beside = beside + padded[:, :, 1:-1, 2:, 1:-1] + padded[:, :, 1:-1, :-2, 1:-1]
    beside = beside + padded[:, :, 1:-1, 1:-1, 2:] + padded[:, :, 1:-1, 1:-1, :-2]
    return wide + (beside - 6.0 * center)


def butterfly_sum(x, axis):
    count = lax.axis_size(axis)
    if count & (count - 1):
        return lax.psum(x, axis)
    step = 1
    while step < count:
        x = x + lax.ppermute(x, axis, [(i, i ^ step) for i in range(count)])
        step *= 2
    return x


def butterfly_gather(x, axis, dim):
    count = lax.axis_size(axis)
    if count & (count - 1):
        return lax.all_gather(x, axis, axis=dim, tiled=True)
    index = lax.axis_index(axis)
    step = 1
    while step < count:
        other = lax.ppermute(x, axis, [(i, i ^ step) for i in range(count)])
        low = (index // step) % 2 == 0
        x = jnp.where(low, jnp.concatenate([x, other], dim), jnp.concatenate([other, x], dim))
        step *= 2
    return x


def expand_rows(coeffs_t):
    count = coeffs_t.shape[0]
    first, second = np.triu_indices(count)
    quad = jnp.take(coeffs_t, first, axis=0) * jnp.take(coeffs_t, second, axis=0)
    ones = jnp.ones((1, coeffs_t.shape[1]), coeffs_t.dtype)
    return jnp.concatenate([ones, coeffs_t, quad], axis=0)


def body(snapshots, picks, basis, kappa):
    modes = basis.shape[0]
    adjoint = adjoint_basis(basis, kappa).reshape(modes, -1)
    stored = snapshots.shape[0]
    flat = snapshots.reshape(stored, -1).astype(jnp.float32)
    partial_t = lax.dot_general(
        adjoint,
        flat,
        (((1,), (1,)), ((), ())),
        precision=lax.Precision.HIGHEST,
        preferred_element_type=jnp.float32,
    )
    part_t = jnp.take(partial_t, picks, axis=1)
    own_t = butterfly_sum(part_t, "space")
    coeffs_t = butterfly_gather(own_t, "tm", 1)
    features_t = expand_rows(coeffs_t)
    gram = lax.dot_general(
        features_t,
        features_t,
        (((1,), (1,)), ((), ())),
        precision=lax.Precision.HIGHEST,
        preferred_element_type=jnp.float32,
    ) / coeffs_t.shape[1]
    factor = cholesky_upper(gram)
    return (own_t.T, factor)


def solution(mesh):
    in_specs = (
        P("tm", None, "space", None, None),
        P("tm"),
        P(None, None, "space", None, None),
        P(None, "space", None, None),
    )
    out_specs = (P("tm", None), P())
    return jax.shard_map(body, mesh=mesh, in_specs=in_specs, out_specs=out_specs, check_vma=False)
```

```python
import functools

import jax
import jax.numpy as jnp
import numpy as np
from jax import lax
from jax.experimental import pallas as pl
from jax.experimental.pallas import tpu as pltpu
from jax.sharding import PartitionSpec as P

PANEL = 128


def split3(x):
    hi = x.astype(jnp.bfloat16)
    rest = x - hi.astype(jnp.float32)
    mid = rest.astype(jnp.bfloat16)
    lo = (rest - mid.astype(jnp.float32)).astype(jnp.bfloat16)
    return hi, mid, lo


def dot3(a, b):
    a1, a2, a3 = split3(a)
    b1, b2, b3 = split3(b)
    def d(x, y):
        return jnp.dot(x, y, preferred_element_type=jnp.float32)
    return d(a1, b1) + (d(a1, b2) + d(a2, b1)) + (d(a1, b3) + d(a3, b1) + d(a2, b2))


def chol_kernel(a_ref, r_ref, w_ref, blk_ref, *, size, valid):
    panels = size // PANEL
    r_ref[...] = jnp.zeros((size, size), jnp.float32)
    w_ref[...] = a_ref[...]
    rows = lax.broadcasted_iota(jnp.int32, (PANEL, 2 * PANEL), 0)
    lanes = lax.broadcasted_iota(jnp.int32, (PANEL, 2 * PANEL), 1)
    eye = (rows[:, :PANEL] == lanes[:, :PANEL]).astype(jnp.float32)
    row_lanes = lax.broadcasted_iota(jnp.int32, (1, 2 * PANEL), 1)
    col_rows = lax.broadcasted_iota(jnp.int32, (PANEL, 1), 0)
    for p in range(panels):
        c0 = p * PANEL
        c1 = c0 + PANEL
        steps = min(PANEL, valid - c0)
        blk_ref[:, :PANEL] = w_ref[c0:c1, c0:c1]
        blk_ref[:, PANEL:] = eye

        def step(j, carry):
            row = blk_ref[pl.ds(j, 1), :]
            pivot = jnp.sum(jnp.where(row_lanes[:, :PANEL] == j, row[:, :PANEL], 0.0), axis=1, keepdims=True)
            scaled = row * lax.rsqrt(pivot)
            column = jnp.transpose(jnp.broadcast_to(scaled[:, :PANEL], (8, PANEL)))[:, 0:1]
            coef = jnp.where(col_rows > j, column, 0.0)
            blk_ref[...] = blk_ref[...] - coef * scaled
            blk_ref[pl.ds(j, 1), :] = scaled
            return carry

        lax.fori_loop(0, steps, step, 0)
        block = blk_ref[...]
        upper = jnp.where(lanes[:, :PANEL] >= rows[:, :PANEL], block[:, :PANEL], 0.0)
        r_ref[c0:c1, c0:c1] = upper
        if p + 1 < panels:
            inv_t = block[:, PANEL:]
            right = dot3(inv_t, w_ref[c0:c1, c1:size])
            r_ref[c0:c1, c1:size] = right
            w_ref[c1:size, c1:size] = w_ref[c1:size, c1:size] - dot3(right.T, right)


def cholesky_upper(gram):
    n = gram.shape[0]
    size = -(-n // PANEL) * PANEL
    padded = jnp.pad(gram, ((0, size - n), (0, size - n)))
    fill = (jnp.arange(size) >= n).astype(jnp.float32)
    padded = padded + jnp.diag(fill)
    out = pl.pallas_call(
        functools.partial(chol_kernel, size=size, valid=n),
        out_shape=jax.ShapeDtypeStruct((size, size), jnp.float32),
        scratch_shapes=[pltpu.VMEM((size, size), jnp.float32), pltpu.VMEM((PANEL, 2 * PANEL), jnp.float32)],
    )(padded)
    return out[:n, :n]


def neighbour_planes(block, axis, dim):
    count = lax.axis_size(axis)
    forward = [(i, i + 1) for i in range(count - 1)]
    backward = [(target, source) for source, target in forward]
    width = block.shape[dim]
    low = lax.ppermute(lax.slice_in_dim(block, width - 1, width, axis=dim), axis, forward)
    high = lax.ppermute(lax.slice_in_dim(block, 0, 1, axis=dim), axis, backward)
    return jnp.concatenate([low, block, high], axis=dim)


def adjoint_basis(basis, kappa):
    wide = basis.astype(jnp.float32)
    scaled = kappa[None] * wide
    padded = neighbour_planes(scaled, "space", 2)
    padded = jnp.pad(padded, ((0, 0), (0, 0), (0, 0), (1, 1), (1, 1)))
    center = padded[:, :, 1:-1, 1:-1, 1:-1]
    beside = padded[:, :, 2:, 1:-1, 1:-1] + padded[:, :, :-2, 1:-1, 1:-1]
    beside = beside + padded[:, :, 1:-1, 2:, 1:-1] + padded[:, :, 1:-1, :-2, 1:-1]
    beside = beside + padded[:, :, 1:-1, 1:-1, 2:] + padded[:, :, 1:-1, 1:-1, :-2]
    return wide + (beside - 6.0 * center)


def butterfly_sum(x, axis):
    count = lax.axis_size(axis)
    if count & (count - 1):
        return lax.psum(x, axis)
    step = 1
    while step < count:
        x = x + lax.ppermute(x, axis, [(i, i ^ step) for i in range(count)])
        step *= 2
    return x


def butterfly_gather(x, axis, dim):
    count = lax.axis_size(axis)
    if count & (count - 1):
        return lax.all_gather(x, axis, axis=dim, tiled=True)
    index = lax.axis_index(axis)
    step = 1
    while step < count:
        other = lax.ppermute(x, axis, [(i, i ^ step) for i in range(count)])
        low = (index // step) % 2 == 0
        x = jnp.where(low, jnp.concatenate([x, other], dim), jnp.concatenate([other, x], dim))
        step *= 2
    return x


def expand_rows(coeffs_t):
    count = coeffs_t.shape[0]
    first, second = np.triu_indices(count)
    quad = jnp.take(coeffs_t, first, axis=0) * jnp.take(coeffs_t, second, axis=0)
    ones = jnp.ones((1, coeffs_t.shape[1]), coeffs_t.dtype)
    return jnp.concatenate([ones, coeffs_t, quad], axis=0)


def body(snapshots, picks, basis, kappa):
    modes = basis.shape[0]
    adjoint = adjoint_basis(basis, kappa).reshape(modes, -1)
    stored = snapshots.shape[0]
    flat = snapshots.reshape(stored, -1).astype(jnp.float32)
    partial_t = lax.dot_general(
        adjoint,
        flat,
        (((1,), (1,)), ((), ())),
        precision=lax.Precision.HIGHEST,
        preferred_element_type=jnp.float32,
    )
    part_t = jnp.take(partial_t, picks, axis=1)
    own_t = butterfly_sum(part_t, "space")
    coeffs_t = butterfly_gather(own_t, "tm", 1)
    features_t = expand_rows(coeffs_t)
    gram = lax.dot_general(
        features_t,
        features_t,
        (((1,), (1,)), ((), ())),
        precision=lax.Precision.HIGHEST,
        preferred_element_type=jnp.float32,
    ) / coeffs_t.shape[1]
    factor = cholesky_upper(gram)
    return (own_t.T, factor)


def solution(mesh):
    in_specs = (
        P("tm", None, "space", None, None),
        P("tm"),
        P(None, None, "space", None, None),
        P(None, "space", None, None),
    )
    out_specs = (P("tm", None), P())
    return jax.shard_map(body, mesh=mesh, in_specs=in_specs, out_specs=out_specs, check_vma=False)
```

```python
import functools

import jax
import jax.numpy as jnp
import numpy as np
from jax import lax
from jax.experimental import pallas as pl
from jax.experimental.pallas import tpu as pltpu
from jax.sharding import PartitionSpec as P

PANEL = 128


def split3(x):
    hi = x.astype(jnp.bfloat16)
    rest = x - hi.astype(jnp.float32)
    mid = rest.astype(jnp.bfloat16)
    lo = (rest - mid.astype(jnp.float32)).astype(jnp.bfloat16)
    return hi, mid, lo


def dot3(a, b):
    a1, a2, a3 = split3(a)
    b1, b2, b3 = split3(b)
    def d(x, y):
        return jnp.dot(x, y, preferred_element_type=jnp.float32)
    return d(a1, b1) + (d(a1, b2) + d(a2, b1)) + (d(a1, b3) + d(a3, b1) + d(a2, b2))


def chol_kernel(a_ref, r_ref, w_ref, blk_ref, *, size, valid):
    panels = size // PANEL
    r_ref[...] = jnp.zeros((size, size), jnp.float32)
    w_ref[...] = a_ref[...]
    rows = lax.broadcasted_iota(jnp.int32, (PANEL, 2 * PANEL), 0)
    lanes = lax.broadcasted_iota(jnp.int32, (PANEL, 2 * PANEL), 1)
    eye = (rows[:, :PANEL] == lanes[:, :PANEL]).astype(jnp.float32)
    group_lanes = lax.broadcasted_iota(jnp.int32, (8, PANEL), 1)
    group_rows = lax.broadcasted_iota(jnp.int32, (8, 1), 0)
    col_rows = lax.broadcasted_iota(jnp.int32, (PANEL, 1), 0)
    for p in range(panels):
        c0 = p * PANEL
        c1 = c0 + PANEL
        groups = -(-min(PANEL, valid - c0) // 8)
        blk_ref[:, :PANEL] = w_ref[c0:c1, c0:c1]
        blk_ref[:, PANEL:] = eye

        def group_step(g, carry):
            base = pl.multiple_of(g * 8, 8)
            eight = blk_ref[pl.ds(base, 8), :]
            for i in range(8):
                j = base + i
                row = eight[i : i + 1, :]
                hit = group_lanes == j
                pivot = jnp.sum(jnp.where(hit[:1], row[:, :PANEL], 0.0), axis=1, keepdims=True)
                scale = lax.rsqrt(pivot)
                scaled = row * scale
                column = jnp.sum(jnp.where(hit, eight[:, :PANEL], 0.0), axis=1, keepdims=True)
                coef = jnp.where(group_rows > i, column * scale, 0.0)
                eight = jnp.where(group_rows == i, scaled, eight - coef * scaled)
            blk_ref[pl.ds(base, 8), :] = eight
            lead = jnp.transpose(eight[:, :PANEL])
            lead = jnp.where(col_rows >= base + 8, lead, 0.0)
            block = blk_ref[...]
            for i in range(8):
                block = block - lead[:, i : i + 1] * eight[i : i + 1, :]
            blk_ref[...] = block
            return carry

        lax.fori_loop(0, groups, group_step, 0)
        block = blk_ref[...]
        upper = jnp.where(lanes[:, :PANEL] >= rows[:, :PANEL], block[:, :PANEL], 0.0)
        r_ref[c0:c1, c0:c1] = upper
        if p + 1 < panels:
            inv_t = block[:, PANEL:]
            right = dot3(inv_t, w_ref[c0:c1, c1:size])
            r_ref[c0:c1, c1:size] = right
            w_ref[c1:size, c1:size] = w_ref[c1:size, c1:size] - dot3(right.T, right)


def cholesky_upper(gram):
    n = gram.shape[0]
    size = -(-n // PANEL) * PANEL
    padded = jnp.pad(gram, ((0, size - n), (0, size - n)))
    fill = (jnp.arange(size) >= n).astype(jnp.float32)
    padded = padded + jnp.diag(fill)
    out = pl.pallas_call(
        functools.partial(chol_kernel, size=size, valid=n),
        out_shape=jax.ShapeDtypeStruct((size, size), jnp.float32),
        scratch_shapes=[pltpu.VMEM((size, size), jnp.float32), pltpu.VMEM((PANEL, 2 * PANEL), jnp.float32)],
    )(padded)
    return out[:n, :n]


def neighbour_planes(block, axis, dim):
    count = lax.axis_size(axis)
    forward = [(i, i + 1) for i in range(count - 1)]
    backward = [(target, source) for source, target in forward]
    width = block.shape[dim]
    low = lax.ppermute(lax.slice_in_dim(block, width - 1, width, axis=dim), axis, forward)
    high = lax.ppermute(lax.slice_in_dim(block, 0, 1, axis=dim), axis, backward)
    return jnp.concatenate([low, block, high], axis=dim)


def adjoint_basis(basis, kappa):
    wide = basis.astype(jnp.float32)
    scaled = kappa[None] * wide
    padded = neighbour_planes(scaled, "space", 2)
    padded = jnp.pad(padded, ((0, 0), (0, 0), (0, 0), (1, 1), (1, 1)))
    center = padded[:, :, 1:-1, 1:-1, 1:-1]
    beside = padded[:, :, 2:, 1:-1, 1:-1] + padded[:, :, :-2, 1:-1, 1:-1]
    beside = beside + padded[:, :, 1:-1, 2:, 1:-1] + padded[:, :, 1:-1, :-2, 1:-1]
    beside = beside + padded[:, :, 1:-1, 1:-1, 2:] + padded[:, :, 1:-1, 1:-1, :-2]
    return wide + (beside - 6.0 * center)


def butterfly_sum(x, axis):
    count = lax.axis_size(axis)
    if count & (count - 1):
        return lax.psum(x, axis)
    step = 1
    while step < count:
        x = x + lax.ppermute(x, axis, [(i, i ^ step) for i in range(count)])
        step *= 2
    return x


def butterfly_gather(x, axis, dim):
    count = lax.axis_size(axis)
    if count & (count - 1):
        return lax.all_gather(x, axis, axis=dim, tiled=True)
    index = lax.axis_index(axis)
    step = 1
    while step < count:
        other = lax.ppermute(x, axis, [(i, i ^ step) for i in range(count)])
        low = (index // step) % 2 == 0
        x = jnp.where(low, jnp.concatenate([x, other], dim), jnp.concatenate([other, x], dim))
        step *= 2
    return x


def expand_rows(coeffs_t):
    count = coeffs_t.shape[0]
    first, second = np.triu_indices(count)
    quad = jnp.take(coeffs_t, first, axis=0) * jnp.take(coeffs_t, second, axis=0)
    ones = jnp.ones((1, coeffs_t.shape[1]), coeffs_t.dtype)
    return jnp.concatenate([ones, coeffs_t, quad], axis=0)


def body(snapshots, picks, basis, kappa):
    modes = basis.shape[0]
    adjoint = adjoint_basis(basis, kappa).reshape(modes, -1)
    stored = snapshots.shape[0]
    flat = snapshots.reshape(stored, -1).astype(jnp.float32)
    partial_t = lax.dot_general(
        adjoint,
        flat,
        (((1,), (1,)), ((), ())),
        precision=lax.Precision.HIGHEST,
        preferred_element_type=jnp.float32,
    )
    part_t = jnp.take(partial_t, picks, axis=1)
    own_t = butterfly_sum(part_t, "space")
    coeffs_t = butterfly_gather(own_t, "tm", 1)
    features_t = expand_rows(coeffs_t)
    gram = lax.dot_general(
        features_t,
        features_t,
        (((1,), (1,)), ((), ())),
        precision=lax.Precision.HIGHEST,
        preferred_element_type=jnp.float32,
    ) / coeffs_t.shape[1]
    factor = cholesky_upper(gram)
    return (own_t.T, factor)


def solution(mesh):
    in_specs = (
        P("tm", None, "space", None, None),
        P("tm"),
        P(None, None, "space", None, None),
        P(None, "space", None, None),
    )
    out_specs = (P("tm", None), P())
    return jax.shard_map(body, mesh=mesh, in_specs=in_specs, out_specs=out_specs, check_vma=False)
```

```python
import functools

import jax
import jax.numpy as jnp
import numpy as np
from jax import lax
from jax.experimental import pallas as pl
from jax.experimental.pallas import tpu as pltpu
from jax.sharding import PartitionSpec as P

PANEL = 128


def split3(x):
    hi = x.astype(jnp.bfloat16)
    rest = x - hi.astype(jnp.float32)
    mid = rest.astype(jnp.bfloat16)
    lo = (rest - mid.astype(jnp.float32)).astype(jnp.bfloat16)
    return hi, mid, lo


def dot3(a, b):
    a1, a2, a3 = split3(a)
    b1, b2, b3 = split3(b)
    def d(x, y):
        return jnp.dot(x, y, preferred_element_type=jnp.float32)
    return d(a1, b1) + (d(a1, b2) + d(a2, b1)) + (d(a1, b3) + d(a3, b1) + d(a2, b2))


def chol_kernel(a_ref, r_ref, w_ref, blk_ref, *, size, valid):
    panels = size // PANEL
    r_ref[...] = jnp.zeros((size, size), jnp.float32)
    w_ref[...] = a_ref[...]
    rows = lax.broadcasted_iota(jnp.int32, (PANEL, 2 * PANEL), 0)
    lanes = lax.broadcasted_iota(jnp.int32, (PANEL, 2 * PANEL), 1)
    eye = (rows[:, :PANEL] == lanes[:, :PANEL]).astype(jnp.float32)
    row_lanes = lax.broadcasted_iota(jnp.int32, (1, 2 * PANEL), 1)
    col_rows = lax.broadcasted_iota(jnp.int32, (PANEL, 1), 0)
    for p in range(panels):
        c0 = p * PANEL
        c1 = c0 + PANEL
        steps = min(PANEL, valid - c0)
        blk_ref[:, :PANEL] = w_ref[c0:c1, c0:c1]
        blk_ref[:, PANEL:] = eye

        def step(j, carry):
            row = blk_ref[pl.ds(j, 1), :]
            pivot = jnp.sum(jnp.where(row_lanes == j, row, 0.0), axis=1, keepdims=True)
            scale = lax.rsqrt(pivot)
            scaled = row * scale
            block = blk_ref[...]
            column = jnp.sum(jnp.where(lanes[:, :PANEL] == j, block[:, :PANEL], 0.0), axis=1, keepdims=True)
            coef = jnp.where(col_rows > j, column * scale, 0.0)
            updated = block - coef * scaled
            blk_ref[...] = jnp.where(rows == j, scaled, updated)
            return carry

        lax.fori_loop(0, steps, step, 0)
        block = blk_ref[...]
        upper = jnp.where(lanes[:, :PANEL] >= rows[:, :PANEL], block[:, :PANEL], 0.0)
        r_ref[c0:c1, c0:c1] = upper
        if p + 1 < panels:
            inv_t = block[:, PANEL:]
            right = dot3(inv_t, w_ref[c0:c1, c1:size])
            r_ref[c0:c1, c1:size] = right
            w_ref[c1:size, c1:size] = w_ref[c1:size, c1:size] - dot3(right.T, right)


def cholesky_upper(gram):
    n = gram.shape[0]
    size = -(-n // PANEL) * PANEL
    padded = jnp.pad(gram, ((0, size - n), (0, size - n)))
    fill = (jnp.arange(size) >= n).astype(jnp.float32)
    padded = padded + jnp.diag(fill)
    out = pl.pallas_call(
        functools.partial(chol_kernel, size=size, valid=n),
        out_shape=jax.ShapeDtypeStruct((size, size), jnp.float32),
        scratch_shapes=[pltpu.VMEM((size, size), jnp.float32), pltpu.VMEM((PANEL, 2 * PANEL), jnp.float32)],
    )(padded)
    return out[:n, :n]


def neighbour_planes(block, axis, dim):
    count = lax.axis_size(axis)
    forward = [(i, i + 1) for i in range(count - 1)]
    backward = [(target, source) for source, target in forward]
    width = block.shape[dim]
    low = lax.ppermute(lax.slice_in_dim(block, width - 1, width, axis=dim), axis, forward)
    high = lax.ppermute(lax.slice_in_dim(block, 0, 1, axis=dim), axis, backward)
    return low, high


def interior_adjoint(basis, kappa):
    wide = basis.astype(jnp.float32)
    scaled = kappa[None] * wide
    padded = jnp.pad(scaled, ((0, 0), (0, 0), (1, 1), (1, 1), (1, 1)))
    center = padded[:, :, 1:-1, 1:-1, 1:-1]
    beside = padded[:, :, 2:, 1:-1, 1:-1] + padded[:, :, :-2, 1:-1, 1:-1]
    beside = beside + padded[:, :, 1:-1, 2:, 1:-1] + padded[:, :, 1:-1, :-2, 1:-1]
    beside = beside + padded[:, :, 1:-1, 1:-1, 2:] + padded[:, :, 1:-1, 1:-1, :-2]
    return wide + (beside - 6.0 * center), scaled


def butterfly_sum(x, axis):
    count = lax.axis_size(axis)
    if count & (count - 1):
        return lax.psum(x, axis)
    step = 1
    while step < count:
        x = x + lax.ppermute(x, axis, [(i, i ^ step) for i in range(count)])
        step *= 2
    return x


def butterfly_gather(x, axis, dim):
    count = lax.axis_size(axis)
    if count & (count - 1):
        return lax.all_gather(x, axis, axis=dim, tiled=True)
    index = lax.axis_index(axis)
    step = 1
    while step < count:
        other = lax.ppermute(x, axis, [(i, i ^ step) for i in range(count)])
        low = (index // step) % 2 == 0
        x = jnp.where(low, jnp.concatenate([x, other], dim), jnp.concatenate([other, x], dim))
        step *= 2
    return x


def expand_rows(coeffs_t):
    count = coeffs_t.shape[0]
    first, second = np.triu_indices(count)
    quad = jnp.take(coeffs_t, first, axis=0) * jnp.take(coeffs_t, second, axis=0)
    ones = jnp.ones((1, coeffs_t.shape[1]), coeffs_t.dtype)
    return jnp.concatenate([ones, coeffs_t, quad], axis=0)


def project(left, right):
    return lax.dot_general(
        left,
        right,
        (((1,), (1,)), ((), ())),
        precision=lax.Precision.HIGHEST,
        preferred_element_type=jnp.float32,
    )


def body(snapshots, picks, basis, kappa):
    modes = basis.shape[0]
    stored = snapshots.shape[0]
    inner, scaled = interior_adjoint(basis, kappa)
    low, high = neighbour_planes(scaled, "space", 2)
    flat = snapshots.reshape(stored, -1).astype(jnp.float32)
    partial_t = project(inner.reshape(modes, -1), flat)
    first = snapshots[:, :, 0].reshape(stored, -1).astype(jnp.float32)
    last = snapshots[:, :, -1].reshape(stored, -1).astype(jnp.float32)
    edges = project(low.reshape(modes, -1), first) + project(high.reshape(modes, -1), last)
    partial_t = partial_t + edges
    part_t = jnp.take(partial_t, picks, axis=1)
    own_t = butterfly_sum(part_t, "space")
    coeffs_t = butterfly_gather(own_t, "tm", 1)
    features_t = expand_rows(coeffs_t)
    gram = lax.dot_general(
        features_t,
        features_t,
        (((1,), (1,)), ((), ())),
        precision=lax.Precision.HIGHEST,
        preferred_element_type=jnp.float32,
    ) / coeffs_t.shape[1]
    factor = cholesky_upper(gram)
    return (own_t.T, factor)


def solution(mesh):
    in_specs = (
        P("tm", None, "space", None, None),
        P("tm"),
        P(None, None, "space", None, None),
        P(None, "space", None, None),
    )
    out_specs = (P("tm", None), P())
    return jax.shard_map(body, mesh=mesh, in_specs=in_specs, out_specs=out_specs, check_vma=False)
```

```python
import functools

import jax
import jax.numpy as jnp
import numpy as np
from jax import lax
from jax.experimental import pallas as pl
from jax.experimental.pallas import tpu as pltpu
from jax.sharding import PartitionSpec as P

PANEL = 128


def split3(x):
    hi = x.astype(jnp.bfloat16)
    rest = x - hi.astype(jnp.float32)
    mid = rest.astype(jnp.bfloat16)
    lo = (rest - mid.astype(jnp.float32)).astype(jnp.bfloat16)
    return hi, mid, lo


def dot3(a, b):
    a1, a2, a3 = split3(a)
    b1, b2, b3 = split3(b)
    def d(x, y):
        return jnp.dot(x, y, preferred_element_type=jnp.float32)
    return d(a1, b1) + (d(a1, b2) + d(a2, b1)) + (d(a1, b3) + d(a3, b1) + d(a2, b2))


def chol_kernel(a_ref, r_ref, w_ref, blk_ref, *, size, valid):
    panels = size // PANEL
    r_ref[...] = jnp.zeros((size, size), jnp.float32)
    w_ref[...] = a_ref[...]
    rows = lax.broadcasted_iota(jnp.int32, (PANEL, 2 * PANEL), 0)
    lanes = lax.broadcasted_iota(jnp.int32, (PANEL, 2 * PANEL), 1)
    eye = (rows[:, :PANEL] == lanes[:, :PANEL]).astype(jnp.float32)
    row_lanes = lax.broadcasted_iota(jnp.int32, (1, 2 * PANEL), 1)
    col_rows = lax.broadcasted_iota(jnp.int32, (PANEL, 1), 0)
    for p in range(panels):
        c0 = p * PANEL
        c1 = c0 + PANEL
        steps = min(PANEL, valid - c0)
        blk_ref[:, :PANEL] = w_ref[c0:c1, c0:c1]
        blk_ref[:, PANEL:] = eye

        def step(j, carry):
            row = blk_ref[pl.ds(j, 1), :]
            pivot = jnp.sum(jnp.where(row_lanes[:, :PANEL] == j, row[:, :PANEL], 0.0), axis=1, keepdims=True)
            scale = lax.rsqrt(pivot)
            scaled = row * scale
            block = blk_ref[...]
            column = jnp.sum(jnp.where(lanes[:, :PANEL] == j, block[:, :PANEL], 0.0), axis=1, keepdims=True)
            coef = jnp.where(col_rows > j, column * scale, 0.0)
            blk_ref[...] = block - coef * scaled
            blk_ref[pl.ds(j, 1), :] = scaled
            return carry

        lax.fori_loop(0, steps, step, 0)
        block = blk_ref[...]
        upper = jnp.where(lanes[:, :PANEL] >= rows[:, :PANEL], block[:, :PANEL], 0.0)
        r_ref[c0:c1, c0:c1] = upper
        if p + 1 < panels:
            inv_t = block[:, PANEL:]
            right = dot3(inv_t, w_ref[c0:c1, c1:size])
            r_ref[c0:c1, c1:size] = right
            w_ref[c1:size, c1:size] = w_ref[c1:size, c1:size] - dot3(right.T, right)


def cholesky_upper(gram):
    n = gram.shape[0]
    size = -(-n // PANEL) * PANEL
    padded = jnp.pad(gram, ((0, size - n), (0, size - n)))
    fill = (jnp.arange(size) >= n).astype(jnp.float32)
    padded = padded + jnp.diag(fill)
    out = pl.pallas_call(
        functools.partial(chol_kernel, size=size, valid=n),
        out_shape=jax.ShapeDtypeStruct((size, size), jnp.float32),
        scratch_shapes=[pltpu.VMEM((size, size), jnp.float32), pltpu.VMEM((PANEL, 2 * PANEL), jnp.float32)],
    )(padded)
    return out[:n, :n]


def neighbour_planes(block, axis, dim):
    count = lax.axis_size(axis)
    forward = [(i, i + 1) for i in range(count - 1)]
    backward = [(target, source) for source, target in forward]
    width = block.shape[dim]
    low = lax.ppermute(lax.slice_in_dim(block, width - 1, width, axis=dim), axis, forward)
    high = lax.ppermute(lax.slice_in_dim(block, 0, 1, axis=dim), axis, backward)
    return low, high


def interior_adjoint(basis, kappa):
    wide = basis.astype(jnp.float32)
    scaled = kappa[None] * wide
    padded = jnp.pad(scaled, ((0, 0), (0, 0), (1, 1), (1, 1), (1, 1)))
    center = padded[:, :, 1:-1, 1:-1, 1:-1]
    beside = padded[:, :, 2:, 1:-1, 1:-1] + padded[:, :, :-2, 1:-1, 1:-1]
    beside = beside + padded[:, :, 1:-1, 2:, 1:-1] + padded[:, :, 1:-1, :-2, 1:-1]
    beside = beside + padded[:, :, 1:-1, 1:-1, 2:] + padded[:, :, 1:-1, 1:-1, :-2]
    return wide + (beside - 6.0 * center), scaled


def butterfly_sum(x, axis):
    count = lax.axis_size(axis)
    if count & (count - 1):
        return lax.psum(x, axis)
    step = 1
    while step < count:
        x = x + lax.ppermute(x, axis, [(i, i ^ step) for i in range(count)])
        step *= 2
    return x


def butterfly_gather(x, axis, dim):
    count = lax.axis_size(axis)
    if count & (count - 1):
        return lax.all_gather(x, axis, axis=dim, tiled=True)
    index = lax.axis_index(axis)
    step = 1
    while step < count:
        other = lax.ppermute(x, axis, [(i, i ^ step) for i in range(count)])
        low = (index // step) % 2 == 0
        x = jnp.where(low, jnp.concatenate([x, other], dim), jnp.concatenate([other, x], dim))
        step *= 2
    return x


def expand_rows(coeffs_t):
    count = coeffs_t.shape[0]
    first, second = np.triu_indices(count)
    quad = jnp.take(coeffs_t, first, axis=0) * jnp.take(coeffs_t, second, axis=0)
    ones = jnp.ones((1, coeffs_t.shape[1]), coeffs_t.dtype)
    return jnp.concatenate([ones, coeffs_t, quad], axis=0)


def project(left, right):
    return lax.dot_general(
        left,
        right,
        (((1,), (1,)), ((), ())),
        precision=lax.Precision.HIGHEST,
        preferred_element_type=jnp.float32,
    )


def body(snapshots, picks, basis, kappa):
    modes = basis.shape[0]
    stored = snapshots.shape[0]
    inner, scaled = interior_adjoint(basis, kappa)
    low, high = neighbour_planes(scaled, "space", 2)
    flat = snapshots.reshape(stored, -1).astype(jnp.float32)
    partial_t = project(inner.reshape(modes, -1), flat)
    first = snapshots[:, :, 0].reshape(stored, -1).astype(jnp.float32)
    last = snapshots[:, :, -1].reshape(stored, -1).astype(jnp.float32)
    edges = project(low.reshape(modes, -1), first) + project(high.reshape(modes, -1), last)
    partial_t = partial_t + edges
    part_t = jnp.take(partial_t, picks, axis=1)
    own_t = butterfly_sum(part_t, "space")
    coeffs_t = butterfly_gather(own_t, "tm", 1)
    features_t = expand_rows(coeffs_t)
    gram = lax.dot_general(
        features_t,
        features_t,
        (((1,), (1,)), ((), ())),
        precision=lax.Precision.HIGHEST,
        preferred_element_type=jnp.float32,
    ) / coeffs_t.shape[1]
    factor = cholesky_upper(gram)
    return (own_t.T, factor)


def solution(mesh):
    in_specs = (
        P("tm", None, "space", None, None),
        P("tm"),
        P(None, None, "space", None, None),
        P(None, "space", None, None),
    )
    out_specs = (P("tm", None), P())
    return jax.shard_map(body, mesh=mesh, in_specs=in_specs, out_specs=out_specs, check_vma=False)
```

```python
import functools

import jax
import jax.numpy as jnp
import numpy as np
from jax import lax
from jax.experimental import pallas as pl
from jax.experimental.pallas import tpu as pltpu
from jax.sharding import PartitionSpec as P

PANEL = 128


def split3(x):
    hi = x.astype(jnp.bfloat16)
    rest = x - hi.astype(jnp.float32)
    mid = rest.astype(jnp.bfloat16)
    lo = (rest - mid.astype(jnp.float32)).astype(jnp.bfloat16)
    return hi, mid, lo


def dot3(a, b):
    a1, a2, a3 = split3(a)
    b1, b2, b3 = split3(b)
    def d(x, y):
        return jnp.dot(x, y, preferred_element_type=jnp.float32)
    return d(a1, b1) + (d(a1, b2) + d(a2, b1)) + (d(a1, b3) + d(a3, b1) + d(a2, b2))


def chol_kernel(a_ref, r_ref, w_ref, blk_ref, *, size, valid):
    panels = size // PANEL
    r_ref[...] = jnp.zeros((size, size), jnp.float32)
    w_ref[...] = a_ref[...]
    rows = lax.broadcasted_iota(jnp.int32, (PANEL, 2 * PANEL), 0)
    lanes = lax.broadcasted_iota(jnp.int32, (PANEL, 2 * PANEL), 1)
    eye = (rows[:, :PANEL] == lanes[:, :PANEL]).astype(jnp.float32)
    row_lanes = lax.broadcasted_iota(jnp.int32, (1, 2 * PANEL), 1)
    col_rows = lax.broadcasted_iota(jnp.int32, (PANEL, 1), 0)
    for p in range(panels):
        c0 = p * PANEL
        c1 = c0 + PANEL
        steps = min(PANEL, valid - c0)
        blk_ref[:, :PANEL] = w_ref[c0:c1, c0:c1]
        blk_ref[:, PANEL:] = eye

        for first in range(0, steps, 16):
            top = (first // 8) * 8
            height = PANEL - top
            seg_rows = lax.broadcasted_iota(jnp.int32, (height, 1), 0) + top
            seg_lanes = lax.broadcasted_iota(jnp.int32, (height, PANEL), 1)

            def step(j, carry, top=top, seg_rows=seg_rows, seg_lanes=seg_lanes):
                row = blk_ref[pl.ds(j, 1), :]
                pivot = jnp.sum(jnp.where(row_lanes[:, :PANEL] == j, row[:, :PANEL], 0.0), axis=1, keepdims=True)
                scale = lax.rsqrt(pivot)
                scaled = row * scale
                block = blk_ref[top:, :]
                column = jnp.sum(jnp.where(seg_lanes == j, block[:, :PANEL], 0.0), axis=1, keepdims=True)
                coef = jnp.where(seg_rows > j, column * scale, 0.0)
                blk_ref[top:, :] = block - coef * scaled
                blk_ref[pl.ds(j, 1), :] = scaled
                return carry

            lax.fori_loop(first, min(first + 16, steps), step, 0)
        block = blk_ref[...]
        upper = jnp.where(lanes[:, :PANEL] >= rows[:, :PANEL], block[:, :PANEL], 0.0)
        r_ref[c0:c1, c0:c1] = upper
        if p + 1 < panels:
            inv_t = block[:, PANEL:]
            right = dot3(inv_t, w_ref[c0:c1, c1:size])
            r_ref[c0:c1, c1:size] = right
            w_ref[c1:size, c1:size] = w_ref[c1:size, c1:size] - dot3(right.T, right)


def cholesky_upper(gram):
    n = gram.shape[0]
    size = -(-n // PANEL) * PANEL
    padded = jnp.pad(gram, ((0, size - n), (0, size - n)))
    fill = (jnp.arange(size) >= n).astype(jnp.float32)
    padded = padded + jnp.diag(fill)
    out = pl.pallas_call(
        functools.partial(chol_kernel, size=size, valid=n),
        out_shape=jax.ShapeDtypeStruct((size, size), jnp.float32),
        scratch_shapes=[pltpu.VMEM((size, size), jnp.float32), pltpu.VMEM((PANEL, 2 * PANEL), jnp.float32)],
    )(padded)
    return out[:n, :n]


def neighbour_planes(block, axis, dim):
    count = lax.axis_size(axis)
    forward = [(i, i + 1) for i in range(count - 1)]
    backward = [(target, source) for source, target in forward]
    width = block.shape[dim]
    low = lax.ppermute(lax.slice_in_dim(block, width - 1, width, axis=dim), axis, forward)
    high = lax.ppermute(lax.slice_in_dim(block, 0, 1, axis=dim), axis, backward)
    return low, high


def interior_adjoint(basis, kappa):
    wide = basis.astype(jnp.float32)
    scaled = kappa[None] * wide
    padded = jnp.pad(scaled, ((0, 0), (0, 0), (1, 1), (1, 1), (1, 1)))
    center = padded[:, :, 1:-1, 1:-1, 1:-1]
    beside = padded[:, :, 2:, 1:-1, 1:-1] + padded[:, :, :-2, 1:-1, 1:-1]
    beside = beside + padded[:, :, 1:-1, 2:, 1:-1] + padded[:, :, 1:-1, :-2, 1:-1]
    beside = beside + padded[:, :, 1:-1, 1:-1, 2:] + padded[:, :, 1:-1, 1:-1, :-2]
    return wide + (beside - 6.0 * center), scaled


def butterfly_sum(x, axis):
    count = lax.axis_size(axis)
    if count & (count - 1):
        return lax.psum(x, axis)
    step = 1
    while step < count:
        x = x + lax.ppermute(x, axis, [(i, i ^ step) for i in range(count)])
        step *= 2
    return x


def butterfly_gather(x, axis, dim):
    count = lax.axis_size(axis)
    if count & (count - 1):
        return lax.all_gather(x, axis, axis=dim, tiled=True)
    index = lax.axis_index(axis)
    step = 1
    while step < count:
        other = lax.ppermute(x, axis, [(i, i ^ step) for i in range(count)])
        low = (index // step) % 2 == 0
        x = jnp.where(low, jnp.concatenate([x, other], dim), jnp.concatenate([other, x], dim))
        step *= 2
    return x


def expand_rows(coeffs_t):
    count = coeffs_t.shape[0]
    first, second = np.triu_indices(count)
    quad = jnp.take(coeffs_t, first, axis=0) * jnp.take(coeffs_t, second, axis=0)
    ones = jnp.ones((1, coeffs_t.shape[1]), coeffs_t.dtype)
    return jnp.concatenate([ones, coeffs_t, quad], axis=0)


def project(left, right):
    return lax.dot_general(
        left,
        right,
        (((1,), (1,)), ((), ())),
        precision=lax.Precision.HIGHEST,
        preferred_element_type=jnp.float32,
    )


def body(snapshots, picks, basis, kappa):
    modes = basis.shape[0]
    stored = snapshots.shape[0]
    inner, scaled = interior_adjoint(basis, kappa)
    low, high = neighbour_planes(scaled, "space", 2)
    flat = snapshots.reshape(stored, -1).astype(jnp.float32)
    partial_t = project(inner.reshape(modes, -1), flat)
    first = snapshots[:, :, 0].reshape(stored, -1).astype(jnp.float32)
    last = snapshots[:, :, -1].reshape(stored, -1).astype(jnp.float32)
    edges = project(low.reshape(modes, -1), first) + project(high.reshape(modes, -1), last)
    partial_t = partial_t + edges
    part_t = jnp.take(partial_t, picks, axis=1)
    own_t = butterfly_sum(part_t, "space")
    coeffs_t = butterfly_gather(own_t, "tm", 1)
    features_t = expand_rows(coeffs_t)
    gram = lax.dot_general(
        features_t,
        features_t,
        (((1,), (1,)), ((), ())),
        precision=lax.Precision.HIGHEST,
        preferred_element_type=jnp.float32,
    ) / coeffs_t.shape[1]
    factor = cholesky_upper(gram)
    return (own_t.T, factor)


def solution(mesh):
    in_specs = (
        P("tm", None, "space", None, None),
        P("tm"),
        P(None, None, "space", None, None),
        P(None, "space", None, None),
    )
    out_specs = (P("tm", None), P())
    return jax.shard_map(body, mesh=mesh, in_specs=in_specs, out_specs=out_specs, check_vma=False)
```

```python
import functools

import jax
import jax.numpy as jnp
import numpy as np
from jax import lax
from jax.experimental import pallas as pl
from jax.experimental.pallas import tpu as pltpu
from jax.sharding import PartitionSpec as P

PANEL = 128


def split3(x):
    hi = x.astype(jnp.bfloat16)
    rest = x - hi.astype(jnp.float32)
    mid = rest.astype(jnp.bfloat16)
    lo = (rest - mid.astype(jnp.float32)).astype(jnp.bfloat16)
    return hi, mid, lo


def dot3(a, b):
    a1, a2, a3 = split3(a)
    b1, b2, b3 = split3(b)
    def d(x, y):
        return jnp.dot(x, y, preferred_element_type=jnp.float32)
    return d(a1, b1) + (d(a1, b2) + d(a2, b1)) + (d(a1, b3) + d(a3, b1) + d(a2, b2))


def chol_kernel(a_ref, r_ref, w_ref, blk_ref, *, size, valid):
    panels = size // PANEL
    r_ref[...] = jnp.zeros((size, size), jnp.float32)
    w_ref[...] = a_ref[...]
    rows = lax.broadcasted_iota(jnp.int32, (PANEL, 2 * PANEL), 0)
    lanes = lax.broadcasted_iota(jnp.int32, (PANEL, 2 * PANEL), 1)
    eye = (rows[:, :PANEL] == lanes[:, :PANEL]).astype(jnp.float32)
    group_rows = lax.broadcasted_iota(jnp.int32, (8, 1), 0)
    for p in range(panels):
        c0 = p * PANEL
        c1 = c0 + PANEL
        steps = min(PANEL, valid - c0)
        blk_ref[:, :PANEL] = w_ref[c0:c1, c0:c1]
        blk_ref[:, PANEL:] = eye
        groups = [blk_ref[8 * g : 8 * g + 8, :] for g in range(PANEL // 8)]
        for j in range(steps):
            own, at = divmod(j, 8)
            row = groups[own][at : at + 1, :]
            scale = lax.rsqrt(row[:, j : j + 1])
            scaled = row * scale
            for g in range(own, PANEL // 8):
                column = groups[g][:, j : j + 1]
                if g == own:
                    coef = jnp.where(group_rows > at, column * scale, 0.0)
                    updated = groups[g] - coef * scaled
                    groups[g] = jnp.where(group_rows == at, scaled, updated)
                else:
                    groups[g] = groups[g] - (column * scale) * scaled
        for g in range(PANEL // 8):
            blk_ref[8 * g : 8 * g + 8, :] = groups[g]
        block = blk_ref[...]
        upper = jnp.where(lanes[:, :PANEL] >= rows[:, :PANEL], block[:, :PANEL], 0.0)
        r_ref[c0:c1, c0:c1] = upper
        if p + 1 < panels:
            inv_t = block[:, PANEL:]
            right = dot3(inv_t, w_ref[c0:c1, c1:size])
            r_ref[c0:c1, c1:size] = right
            w_ref[c1:size, c1:size] = w_ref[c1:size, c1:size] - dot3(right.T, right)


def cholesky_upper(gram):
    n = gram.shape[0]
    size = -(-n // PANEL) * PANEL
    padded = jnp.pad(gram, ((0, size - n), (0, size - n)))
    fill = (jnp.arange(size) >= n).astype(jnp.float32)
    padded = padded + jnp.diag(fill)
    out = pl.pallas_call(
        functools.partial(chol_kernel, size=size, valid=n),
        out_shape=jax.ShapeDtypeStruct((size, size), jnp.float32),
        scratch_shapes=[pltpu.VMEM((size, size), jnp.float32), pltpu.VMEM((PANEL, 2 * PANEL), jnp.float32)],
    )(padded)
    return out[:n, :n]


def neighbour_planes(block, axis, dim):
    count = lax.axis_size(axis)
    forward = [(i, i + 1) for i in range(count - 1)]
    backward = [(target, source) for source, target in forward]
    width = block.shape[dim]
    low = lax.ppermute(lax.slice_in_dim(block, width - 1, width, axis=dim), axis, forward)
    high = lax.ppermute(lax.slice_in_dim(block, 0, 1, axis=dim), axis, backward)
    return low, high


def interior_adjoint(basis, kappa):
    wide = basis.astype(jnp.float32)
    scaled = kappa[None] * wide
    padded = jnp.pad(scaled, ((0, 0), (0, 0), (1, 1), (1, 1), (1, 1)))
    center = padded[:, :, 1:-1, 1:-1, 1:-1]
    beside = padded[:, :, 2:, 1:-1, 1:-1] + padded[:, :, :-2, 1:-1, 1:-1]
    beside = beside + padded[:, :, 1:-1, 2:, 1:-1] + padded[:, :, 1:-1, :-2, 1:-1]
    beside = beside + padded[:, :, 1:-1, 1:-1, 2:] + padded[:, :, 1:-1, 1:-1, :-2]
    return wide + (beside - 6.0 * center), scaled


def butterfly_sum(x, axis):
    count = lax.axis_size(axis)
    if count & (count - 1):
        return lax.psum(x, axis)
    step = 1
    while step < count:
        x = x + lax.ppermute(x, axis, [(i, i ^ step) for i in range(count)])
        step *= 2
    return x


def butterfly_gather(x, axis, dim):
    count = lax.axis_size(axis)
    if count & (count - 1):
        return lax.all_gather(x, axis, axis=dim, tiled=True)
    index = lax.axis_index(axis)
    step = 1
    while step < count:
        other = lax.ppermute(x, axis, [(i, i ^ step) for i in range(count)])
        low = (index // step) % 2 == 0
        x = jnp.where(low, jnp.concatenate([x, other], dim), jnp.concatenate([other, x], dim))
        step *= 2
    return x


def expand_rows(coeffs_t):
    count = coeffs_t.shape[0]
    first, second = np.triu_indices(count)
    quad = jnp.take(coeffs_t, first, axis=0) * jnp.take(coeffs_t, second, axis=0)
    ones = jnp.ones((1, coeffs_t.shape[1]), coeffs_t.dtype)
    return jnp.concatenate([ones, coeffs_t, quad], axis=0)


def project(left, right):
    return lax.dot_general(
        left,
        right,
        (((1,), (1,)), ((), ())),
        precision=lax.Precision.HIGHEST,
        preferred_element_type=jnp.float32,
    )


def body(snapshots, picks, basis, kappa):
    modes = basis.shape[0]
    stored = snapshots.shape[0]
    inner, scaled = interior_adjoint(basis, kappa)
    low, high = neighbour_planes(scaled, "space", 2)
    flat = snapshots.reshape(stored, -1).astype(jnp.float32)
    partial_t = project(inner.reshape(modes, -1), flat)
    first = snapshots[:, :, 0].reshape(stored, -1).astype(jnp.float32)
    last = snapshots[:, :, -1].reshape(stored, -1).astype(jnp.float32)
    edges = project(low.reshape(modes, -1), first) + project(high.reshape(modes, -1), last)
    partial_t = partial_t + edges
    part_t = jnp.take(partial_t, picks, axis=1)
    own_t = butterfly_sum(part_t, "space")
    coeffs_t = butterfly_gather(own_t, "tm", 1)
    features_t = expand_rows(coeffs_t)
    gram = lax.dot_general(
        features_t,
        features_t,
        (((1,), (1,)), ((), ())),
        precision=lax.Precision.HIGHEST,
        preferred_element_type=jnp.float32,
    ) / coeffs_t.shape[1]
    factor = cholesky_upper(gram)
    return (own_t.T, factor)


def solution(mesh):
    in_specs = (
        P("tm", None, "space", None, None),
        P("tm"),
        P(None, None, "space", None, None),
        P(None, "space", None, None),
    )
    out_specs = (P("tm", None), P())
    return jax.shard_map(body, mesh=mesh, in_specs=in_specs, out_specs=out_specs, check_vma=False)
```

```python
import functools

import jax
import jax.numpy as jnp
import numpy as np
from jax import lax
from jax.experimental import pallas as pl
from jax.experimental.pallas import tpu as pltpu
from jax.sharding import PartitionSpec as P

PANEL = 128


def split3(x):
    hi = x.astype(jnp.bfloat16)
    rest = x - hi.astype(jnp.float32)
    mid = rest.astype(jnp.bfloat16)
    lo = (rest - mid.astype(jnp.float32)).astype(jnp.bfloat16)
    return hi, mid, lo


def dot3(a, b):
    a1, a2, a3 = split3(a)
    b1, b2, b3 = split3(b)
    def d(x, y):
        return jnp.dot(x, y, preferred_element_type=jnp.float32)
    return d(a1, b1) + (d(a1, b2) + d(a2, b1)) + (d(a1, b3) + d(a3, b1) + d(a2, b2))


def chol_kernel(a_ref, r_ref, w_ref, blk_ref, *, size, valid):
    panels = size // PANEL
    r_ref[...] = jnp.zeros((size, size), jnp.float32)
    w_ref[...] = a_ref[...]
    rows = lax.broadcasted_iota(jnp.int32, (PANEL, 2 * PANEL), 0)
    lanes = lax.broadcasted_iota(jnp.int32, (PANEL, 2 * PANEL), 1)
    eye = (rows[:, :PANEL] == lanes[:, :PANEL]).astype(jnp.float32)
    group_rows = lax.broadcasted_iota(jnp.int32, (8, 1), 0)
    for p in range(panels):
        c0 = p * PANEL
        c1 = c0 + PANEL
        steps = min(PANEL, valid - c0)
        blk_ref[:, :PANEL] = w_ref[c0:c1, c0:c1]
        blk_ref[:, PANEL:] = eye
        groups = [blk_ref[8 * g : 8 * g + 8, :] for g in range(PANEL // 8)]
        for j in range(steps):
            own, at = divmod(j, 8)
            row = groups[own][at : at + 1, :]
            scale = lax.rsqrt(row[:, j : j + 1])
            scaled = row * scale
            for g in range(own, PANEL // 8):
                column = groups[g][:, j : j + 1]
                if g == own:
                    coef = jnp.where(group_rows > at, column * scale, 0.0)
                    updated = groups[g] - coef * scaled
                    groups[g] = jnp.where(group_rows == at, scaled, updated)
                else:
                    groups[g] = groups[g] - (column * scale) * scaled
        for g in range(PANEL // 8):
            blk_ref[8 * g : 8 * g + 8, :] = groups[g]
        block = blk_ref[...]
        upper = jnp.where(lanes[:, :PANEL] >= rows[:, :PANEL], block[:, :PANEL], 0.0)
        r_ref[c0:c1, c0:c1] = upper
        if p + 1 < panels:
            inv_t = block[:, PANEL:]
            right = dot3(inv_t, w_ref[c0:c1, c1:size])
            r_ref[c0:c1, c1:size] = right
            w_ref[c1:size, c1:size] = w_ref[c1:size, c1:size] - dot3(right.T, right)


def cholesky_upper(gram):
    n = gram.shape[0]
    size = -(-n // PANEL) * PANEL
    padded = jnp.pad(gram, ((0, size - n), (0, size - n)))
    fill = (jnp.arange(size) >= n).astype(jnp.float32)
    padded = padded + jnp.diag(fill)
    out = pl.pallas_call(
        functools.partial(chol_kernel, size=size, valid=n),
        out_shape=jax.ShapeDtypeStruct((size, size), jnp.float32),
        scratch_shapes=[pltpu.VMEM((size, size), jnp.float32), pltpu.VMEM((PANEL, 2 * PANEL), jnp.float32)],
    )(padded)
    return out[:n, :n]


def neighbour_planes(block, axis, dim):
    count = lax.axis_size(axis)
    forward = [(i, i + 1) for i in range(count - 1)]
    backward = [(target, source) for source, target in forward]
    width = block.shape[dim]
    low = lax.ppermute(lax.slice_in_dim(block, width - 1, width, axis=dim), axis, forward)
    high = lax.ppermute(lax.slice_in_dim(block, 0, 1, axis=dim), axis, backward)
    return low, high


def interior_adjoint(basis, kappa):
    wide = basis.astype(jnp.float32)
    scaled = kappa[None] * wide
    padded = jnp.pad(scaled, ((0, 0), (0, 0), (1, 1), (1, 1), (1, 1)))
    center = padded[:, :, 1:-1, 1:-1, 1:-1]
    beside = padded[:, :, 2:, 1:-1, 1:-1] + padded[:, :, :-2, 1:-1, 1:-1]
    beside = beside + padded[:, :, 1:-1, 2:, 1:-1] + padded[:, :, 1:-1, :-2, 1:-1]
    beside = beside + padded[:, :, 1:-1, 1:-1, 2:] + padded[:, :, 1:-1, 1:-1, :-2]
    return wide + (beside - 6.0 * center), scaled


def butterfly_sum(x, axis):
    count = lax.axis_size(axis)
    if count & (count - 1):
        return lax.psum(x, axis)
    step = 1
    while step < count:
        x = x + lax.ppermute(x, axis, [(i, i ^ step) for i in range(count)])
        step *= 2
    return x


def butterfly_gather(x, axis, dim):
    count = lax.axis_size(axis)
    if count & (count - 1):
        return lax.all_gather(x, axis, axis=dim, tiled=True)
    index = lax.axis_index(axis)
    step = 1
    while step < count:
        other = lax.ppermute(x, axis, [(i, i ^ step) for i in range(count)])
        low = (index // step) % 2 == 0
        x = jnp.where(low, jnp.concatenate([x, other], dim), jnp.concatenate([other, x], dim))
        step *= 2
    return x


def exact_parts(x):
    hi = lax.reduce_precision(x, exponent_bits=8, mantissa_bits=7)
    rest = x - hi
    mid = lax.reduce_precision(rest, exponent_bits=8, mantissa_bits=7)
    low = rest - mid
    return [part.astype(jnp.bfloat16) for part in (hi, mid, low)]


def pick_rows(index, parts):
    width = parts[0].shape[0]
    select = (jnp.arange(width, dtype=jnp.int32)[None, :] == jnp.asarray(index)[:, None]).astype(jnp.bfloat16)
    total = jnp.dot(select, parts[0], preferred_element_type=jnp.float32)
    total = total + jnp.dot(select, parts[1], preferred_element_type=jnp.float32)
    return total + jnp.dot(select, parts[2], preferred_element_type=jnp.float32)


def expand_rows(coeffs_t):
    count = coeffs_t.shape[0]
    first, second = np.triu_indices(count)
    ones = jnp.ones((1, coeffs_t.shape[1]), coeffs_t.dtype)
    parts = exact_parts(jnp.concatenate([ones, coeffs_t], axis=0))
    left = np.concatenate([[0], np.arange(1, count + 1), first + 1]).astype(np.int32)
    right = np.concatenate([[0], np.zeros(count, np.int64), second + 1]).astype(np.int32)
    return pick_rows(left, parts) * pick_rows(right, parts)


def project(left, right):
    return lax.dot_general(
        left,
        right,
        (((1,), (1,)), ((), ())),
        precision=lax.Precision.HIGHEST,
        preferred_element_type=jnp.float32,
    )


def body(snapshots, picks, basis, kappa):
    modes = basis.shape[0]
    stored = snapshots.shape[0]
    inner, scaled = interior_adjoint(basis, kappa)
    low, high = neighbour_planes(scaled, "space", 2)
    flat = snapshots.reshape(stored, -1).astype(jnp.float32)
    partial_t = project(inner.reshape(modes, -1), flat)
    first = snapshots[:, :, 0].reshape(stored, -1).astype(jnp.float32)
    last = snapshots[:, :, -1].reshape(stored, -1).astype(jnp.float32)
    edges = project(low.reshape(modes, -1), first) + project(high.reshape(modes, -1), last)
    partial_t = partial_t + edges
    part_t = jnp.take(partial_t, picks, axis=1)
    own_t = butterfly_sum(part_t, "space")
    coeffs_t = butterfly_gather(own_t, "tm", 1)
    features_t = expand_rows(coeffs_t)
    gram = lax.dot_general(
        features_t,
        features_t,
        (((1,), (1,)), ((), ())),
        precision=lax.Precision.HIGHEST,
        preferred_element_type=jnp.float32,
    ) / coeffs_t.shape[1]
    factor = cholesky_upper(gram)
    return (own_t.T, factor)


def solution(mesh):
    in_specs = (
        P("tm", None, "space", None, None),
        P("tm"),
        P(None, None, "space", None, None),
        P(None, "space", None, None),
    )
    out_specs = (P("tm", None), P())
    return jax.shard_map(body, mesh=mesh, in_specs=in_specs, out_specs=out_specs, check_vma=False)
```

```python
import functools

import jax
import jax.numpy as jnp
import numpy as np
from jax import lax
from jax.experimental import pallas as pl
from jax.experimental.pallas import tpu as pltpu
from jax.sharding import PartitionSpec as P

PANEL = 128
UNROLLED = 2


def split3(x):
    hi = x.astype(jnp.bfloat16)
    rest = x - hi.astype(jnp.float32)
    mid = rest.astype(jnp.bfloat16)
    lo = (rest - mid.astype(jnp.float32)).astype(jnp.bfloat16)
    return hi, mid, lo


def dot3(a, b):
    a1, a2, a3 = split3(a)
    b1, b2, b3 = split3(b)
    def d(x, y):
        return jnp.dot(x, y, preferred_element_type=jnp.float32)
    return d(a1, b1) + (d(a1, b2) + d(a2, b1)) + (d(a1, b3) + d(a3, b1) + d(a2, b2))


def chol_kernel(a_ref, r_ref, w_ref, blk_ref, *, size, valid):
    panels = size // PANEL
    r_ref[...] = jnp.zeros((size, size), jnp.float32)
    w_ref[...] = a_ref[...]
    rows = lax.broadcasted_iota(jnp.int32, (PANEL, 2 * PANEL), 0)
    lanes = lax.broadcasted_iota(jnp.int32, (PANEL, 2 * PANEL), 1)
    eye = (rows[:, :PANEL] == lanes[:, :PANEL]).astype(jnp.float32)
    group_rows = lax.broadcasted_iota(jnp.int32, (8, 1), 0)
    row_lanes = lax.broadcasted_iota(jnp.int32, (1, 2 * PANEL), 1)
    for p in range(panels):
        c0 = p * PANEL
        c1 = c0 + PANEL
        steps = min(PANEL, valid - c0)
        blk_ref[:, :PANEL] = w_ref[c0:c1, c0:c1]
        blk_ref[:, PANEL:] = eye
        if p < UNROLLED:
            groups = [blk_ref[8 * g : 8 * g + 8, :] for g in range(PANEL // 8)]
            for j in range(steps):
                own, at = divmod(j, 8)
                row = groups[own][at : at + 1, :]
                scale = lax.rsqrt(row[:, j : j + 1])
                scaled = row * scale
                for g in range(own, PANEL // 8):
                    column = groups[g][:, j : j + 1]
                    if g == own:
                        coef = jnp.where(group_rows > at, column * scale, 0.0)
                        updated = groups[g] - coef * scaled
                        groups[g] = jnp.where(group_rows == at, scaled, updated)
                    else:
                        groups[g] = groups[g] - (column * scale) * scaled
            for g in range(PANEL // 8):
                blk_ref[8 * g : 8 * g + 8, :] = groups[g]
        else:
            for first in range(0, steps, 16):
                top = (first // 8) * 8
                height = PANEL - top
                seg_rows = lax.broadcasted_iota(jnp.int32, (height, 1), 0) + top
                seg_lanes = lax.broadcasted_iota(jnp.int32, (height, PANEL), 1)

                def step(j, carry, top=top, seg_rows=seg_rows, seg_lanes=seg_lanes):
                    row = blk_ref[pl.ds(j, 1), :]
                    pivot = jnp.sum(jnp.where(row_lanes[:, :PANEL] == j, row[:, :PANEL], 0.0), axis=1, keepdims=True)
                    scale = lax.rsqrt(pivot)
                    scaled = row * scale
                    block = blk_ref[top:, :]
                    column = jnp.sum(jnp.where(seg_lanes == j, block[:, :PANEL], 0.0), axis=1, keepdims=True)
                    coef = jnp.where(seg_rows > j, column * scale, 0.0)
                    blk_ref[top:, :] = block - coef * scaled
                    blk_ref[pl.ds(j, 1), :] = scaled
                    return carry

                lax.fori_loop(first, min(first + 16, steps), step, 0)
        block = blk_ref[...]
        upper = jnp.where(lanes[:, :PANEL] >= rows[:, :PANEL], block[:, :PANEL], 0.0)
        r_ref[c0:c1, c0:c1] = upper
        if p + 1 < panels:
            inv_t = block[:, PANEL:]
            right = dot3(inv_t, w_ref[c0:c1, c1:size])
            r_ref[c0:c1, c1:size] = right
            w_ref[c1:size, c1:size] = w_ref[c1:size, c1:size] - dot3(right.T, right)


def cholesky_upper(gram):
    n = gram.shape[0]
    size = -(-n // PANEL) * PANEL
    padded = jnp.pad(gram, ((0, size - n), (0, size - n)))
    fill = (jnp.arange(size) >= n).astype(jnp.float32)
    padded = padded + jnp.diag(fill)
    out = pl.pallas_call(
        functools.partial(chol_kernel, size=size, valid=n),
        out_shape=jax.ShapeDtypeStruct((size, size), jnp.float32),
        scratch_shapes=[pltpu.VMEM((size, size), jnp.float32), pltpu.VMEM((PANEL, 2 * PANEL), jnp.float32)],
    )(padded)
    return out[:n, :n]


def neighbour_planes(block, axis, dim):
    count = lax.axis_size(axis)
    forward = [(i, i + 1) for i in range(count - 1)]
    backward = [(target, source) for source, target in forward]
    width = block.shape[dim]
    low = lax.ppermute(lax.slice_in_dim(block, width - 1, width, axis=dim), axis, forward)
    high = lax.ppermute(lax.slice_in_dim(block, 0, 1, axis=dim), axis, backward)
    return low, high


def interior_adjoint(basis, kappa):
    wide = basis.astype(jnp.float32)
    scaled = kappa[None] * wide
    padded = jnp.pad(scaled, ((0, 0), (0, 0), (1, 1), (1, 1), (1, 1)))
    center = padded[:, :, 1:-1, 1:-1, 1:-1]
    beside = padded[:, :, 2:, 1:-1, 1:-1] + padded[:, :, :-2, 1:-1, 1:-1]
    beside = beside + padded[:, :, 1:-1, 2:, 1:-1] + padded[:, :, 1:-1, :-2, 1:-1]
    beside = beside + padded[:, :, 1:-1, 1:-1, 2:] + padded[:, :, 1:-1, 1:-1, :-2]
    return wide + (beside - 6.0 * center), scaled


def butterfly_sum(x, axis):
    count = lax.axis_size(axis)
    if count & (count - 1):
        return lax.psum(x, axis)
    step = 1
    while step < count:
        x = x + lax.ppermute(x, axis, [(i, i ^ step) for i in range(count)])
        step *= 2
    return x


def butterfly_gather(x, axis, dim):
    count = lax.axis_size(axis)
    if count & (count - 1):
        return lax.all_gather(x, axis, axis=dim, tiled=True)
    index = lax.axis_index(axis)
    step = 1
    while step < count:
        other = lax.ppermute(x, axis, [(i, i ^ step) for i in range(count)])
        low = (index // step) % 2 == 0
        x = jnp.where(low, jnp.concatenate([x, other], dim), jnp.concatenate([other, x], dim))
        step *= 2
    return x


def expand_rows(coeffs_t):
    count = coeffs_t.shape[0]
    first, second = np.triu_indices(count)
    quad = jnp.take(coeffs_t, first, axis=0) * jnp.take(coeffs_t, second, axis=0)
    ones = jnp.ones((1, coeffs_t.shape[1]), coeffs_t.dtype)
    return jnp.concatenate([ones, coeffs_t, quad], axis=0)


def project(left, right):
    return lax.dot_general(
        left,
        right,
        (((1,), (1,)), ((), ())),
        precision=lax.Precision.HIGHEST,
        preferred_element_type=jnp.float32,
    )


def body(snapshots, picks, basis, kappa):
    modes = basis.shape[0]
    stored = snapshots.shape[0]
    inner, scaled = interior_adjoint(basis, kappa)
    low, high = neighbour_planes(scaled, "space", 2)
    flat = snapshots.reshape(stored, -1).astype(jnp.float32)
    partial_t = project(inner.reshape(modes, -1), flat)
    first = snapshots[:, :, 0].reshape(stored, -1).astype(jnp.float32)
    last = snapshots[:, :, -1].reshape(stored, -1).astype(jnp.float32)
    edges = project(low.reshape(modes, -1), first) + project(high.reshape(modes, -1), last)
    partial_t = partial_t + edges
    part_t = jnp.take(partial_t, picks, axis=1)
    own_t = butterfly_sum(part_t, "space")
    coeffs_t = butterfly_gather(own_t, "tm", 1)
    features_t = expand_rows(coeffs_t)
    gram = lax.dot_general(
        features_t,
        features_t,
        (((1,), (1,)), ((), ())),
        precision=lax.Precision.HIGHEST,
        preferred_element_type=jnp.float32,
    ) / coeffs_t.shape[1]
    factor = cholesky_upper(gram)
    return (own_t.T, factor)


def solution(mesh):
    in_specs = (
        P("tm", None, "space", None, None),
        P("tm"),
        P(None, None, "space", None, None),
        P(None, "space", None, None),
    )
    out_specs = (P("tm", None), P())
    return jax.shard_map(body, mesh=mesh, in_specs=in_specs, out_specs=out_specs, check_vma=False)
```

```python
import functools

import jax
import jax.numpy as jnp
import numpy as np
from jax import lax
from jax.experimental import pallas as pl
from jax.experimental.pallas import tpu as pltpu
from jax.sharding import PartitionSpec as P

PANEL = 128
UNROLLED = 2


def split3(x):
    hi = x.astype(jnp.bfloat16)
    rest = x - hi.astype(jnp.float32)
    mid = rest.astype(jnp.bfloat16)
    lo = (rest - mid.astype(jnp.float32)).astype(jnp.bfloat16)
    return hi, mid, lo


def dot3(a, b):
    a1, a2, a3 = split3(a)
    b1, b2, b3 = split3(b)
    def d(x, y):
        return jnp.dot(x, y, preferred_element_type=jnp.float32)
    return d(a1, b1) + (d(a1, b2) + d(a2, b1)) + (d(a1, b3) + d(a3, b1) + d(a2, b2))


def chol_kernel(a_ref, r_ref, w_ref, blk_ref, *, size, valid):
    panels = size // PANEL
    r_ref[...] = jnp.zeros((valid, valid), jnp.float32)
    fill_rows = lax.broadcasted_iota(jnp.int32, (size, size), 0)
    fill_cols = lax.broadcasted_iota(jnp.int32, (size, size), 1)
    w_ref[...] = jnp.where((fill_rows == fill_cols) & (fill_rows >= valid), 1.0, 0.0).astype(jnp.float32)
    w_ref[0:valid, 0:valid] = a_ref[...]
    rows = lax.broadcasted_iota(jnp.int32, (PANEL, 2 * PANEL), 0)
    lanes = lax.broadcasted_iota(jnp.int32, (PANEL, 2 * PANEL), 1)
    eye = (rows[:, :PANEL] == lanes[:, :PANEL]).astype(jnp.float32)
    group_rows = lax.broadcasted_iota(jnp.int32, (8, 1), 0)
    row_lanes = lax.broadcasted_iota(jnp.int32, (1, 2 * PANEL), 1)
    for p in range(panels):
        c0 = p * PANEL
        c1 = c0 + PANEL
        steps = min(PANEL, valid - c0)
        blk_ref[:, :PANEL] = w_ref[c0:c1, c0:c1]
        blk_ref[:, PANEL:] = eye
        if p < UNROLLED:
            groups = [blk_ref[8 * g : 8 * g + 8, :] for g in range(PANEL // 8)]
            for j in range(steps):
                own, at = divmod(j, 8)
                row = groups[own][at : at + 1, :]
                scale = lax.rsqrt(row[:, j : j + 1])
                scaled = row * scale
                for g in range(own, PANEL // 8):
                    column = groups[g][:, j : j + 1]
                    if g == own:
                        coef = jnp.where(group_rows > at, column * scale, 0.0)
                        updated = groups[g] - coef * scaled
                        groups[g] = jnp.where(group_rows == at, scaled, updated)
                    else:
                        groups[g] = groups[g] - (column * scale) * scaled
            for g in range(PANEL // 8):
                blk_ref[8 * g : 8 * g + 8, :] = groups[g]
        else:
            for first in range(0, steps, 16):
                top = (first // 8) * 8
                height = PANEL - top
                seg_rows = lax.broadcasted_iota(jnp.int32, (height, 1), 0) + top
                seg_lanes = lax.broadcasted_iota(jnp.int32, (height, PANEL), 1)

                def step(j, carry, top=top, seg_rows=seg_rows, seg_lanes=seg_lanes):
                    row = blk_ref[pl.ds(j, 1), :]
                    pivot = jnp.sum(jnp.where(row_lanes[:, :PANEL] == j, row[:, :PANEL], 0.0), axis=1, keepdims=True)
                    scale = lax.rsqrt(pivot)
                    scaled = row * scale
                    block = blk_ref[top:, :]
                    column = jnp.sum(jnp.where(seg_lanes == j, block[:, :PANEL], 0.0), axis=1, keepdims=True)
                    coef = jnp.where(seg_rows > j, column * scale, 0.0)
                    blk_ref[top:, :] = block - coef * scaled
                    blk_ref[pl.ds(j, 1), :] = scaled
                    return carry

                lax.fori_loop(first, min(first + 16, steps), step, 0)
        block = blk_ref[...]
        upper = jnp.where(lanes[:, :PANEL] >= rows[:, :PANEL], block[:, :PANEL], 0.0)
        end = min(c1, valid)
        r_ref[c0:end, c0:end] = upper[: end - c0, : end - c0]
        if p + 1 < panels:
            inv_t = block[:, PANEL:]
            right = dot3(inv_t, w_ref[c0:c1, c1:size])
            r_ref[c0:c1, c1:valid] = right[:, : valid - c1]
            w_ref[c1:size, c1:size] = w_ref[c1:size, c1:size] - dot3(right.T, right)


def cholesky_upper(gram):
    n = gram.shape[0]
    size = -(-n // PANEL) * PANEL
    return pl.pallas_call(
        functools.partial(chol_kernel, size=size, valid=n),
        out_shape=jax.ShapeDtypeStruct((n, n), jnp.float32),
        scratch_shapes=[pltpu.VMEM((size, size), jnp.float32), pltpu.VMEM((PANEL, 2 * PANEL), jnp.float32)],
    )(gram)


def neighbour_planes(block, axis, dim):
    count = lax.axis_size(axis)
    forward = [(i, i + 1) for i in range(count - 1)]
    backward = [(target, source) for source, target in forward]
    width = block.shape[dim]
    low = lax.ppermute(lax.slice_in_dim(block, width - 1, width, axis=dim), axis, forward)
    high = lax.ppermute(lax.slice_in_dim(block, 0, 1, axis=dim), axis, backward)
    return low, high


def interior_adjoint(basis, kappa):
    wide = basis.astype(jnp.float32)
    scaled = kappa[None] * wide
    padded = jnp.pad(scaled, ((0, 0), (0, 0), (1, 1), (1, 1), (1, 1)))
    center = padded[:, :, 1:-1, 1:-1, 1:-1]
    beside = padded[:, :, 2:, 1:-1, 1:-1] + padded[:, :, :-2, 1:-1, 1:-1]
    beside = beside + padded[:, :, 1:-1, 2:, 1:-1] + padded[:, :, 1:-1, :-2, 1:-1]
    beside = beside + padded[:, :, 1:-1, 1:-1, 2:] + padded[:, :, 1:-1, 1:-1, :-2]
    return wide + (beside - 6.0 * center), scaled


def butterfly_sum(x, axis):
    count = lax.axis_size(axis)
    if count & (count - 1):
        return lax.psum(x, axis)
    step = 1
    while step < count:
        x = x + lax.ppermute(x, axis, [(i, i ^ step) for i in range(count)])
        step *= 2
    return x


def butterfly_gather(x, axis, dim):
    count = lax.axis_size(axis)
    if count & (count - 1):
        return lax.all_gather(x, axis, axis=dim, tiled=True)
    index = lax.axis_index(axis)
    step = 1
    while step < count:
        other = lax.ppermute(x, axis, [(i, i ^ step) for i in range(count)])
        low = (index // step) % 2 == 0
        x = jnp.where(low, jnp.concatenate([x, other], dim), jnp.concatenate([other, x], dim))
        step *= 2
    return x


def expand_rows(coeffs_t):
    count = coeffs_t.shape[0]
    first, second = np.triu_indices(count)
    quad = jnp.take(coeffs_t, first, axis=0) * jnp.take(coeffs_t, second, axis=0)
    ones = jnp.ones((1, coeffs_t.shape[1]), coeffs_t.dtype)
    return jnp.concatenate([ones, coeffs_t, quad], axis=0)


def project(left, right):
    return lax.dot_general(
        left,
        right,
        (((1,), (1,)), ((), ())),
        precision=lax.Precision.HIGHEST,
        preferred_element_type=jnp.float32,
    )


def body(snapshots, picks, basis, kappa):
    modes = basis.shape[0]
    stored = snapshots.shape[0]
    inner, scaled = interior_adjoint(basis, kappa)
    low, high = neighbour_planes(scaled, "space", 2)
    flat = snapshots.reshape(stored, -1).astype(jnp.float32)
    partial_t = project(inner.reshape(modes, -1), flat)
    first = snapshots[:, :, 0].reshape(stored, -1).astype(jnp.float32)
    last = snapshots[:, :, -1].reshape(stored, -1).astype(jnp.float32)
    edges = project(low.reshape(modes, -1), first) + project(high.reshape(modes, -1), last)
    partial_t = partial_t + edges
    part_t = jnp.take(partial_t, picks, axis=1)
    own_t = butterfly_sum(part_t, "space")
    coeffs_t = butterfly_gather(own_t, "tm", 1)
    features_t = expand_rows(coeffs_t)
    gram = lax.dot_general(
        features_t,
        features_t,
        (((1,), (1,)), ((), ())),
        precision=lax.Precision.HIGHEST,
        preferred_element_type=jnp.float32,
    ) / coeffs_t.shape[1]
    factor = cholesky_upper(gram)
    return (own_t.T, factor)


def solution(mesh):
    in_specs = (
        P("tm", None, "space", None, None),
        P("tm"),
        P(None, None, "space", None, None),
        P(None, "space", None, None),
    )
    out_specs = (P("tm", None), P())
    return jax.shard_map(body, mesh=mesh, in_specs=in_specs, out_specs=out_specs, check_vma=False)
```

```python
import functools

import jax
import jax.numpy as jnp
import numpy as np
from jax import lax
from jax.experimental import pallas as pl
from jax.experimental.pallas import tpu as pltpu
from jax.sharding import PartitionSpec as P

PANEL = 128
UNROLLED = 2


def split3(x):
    hi = x.astype(jnp.bfloat16)
    rest = x - hi.astype(jnp.float32)
    mid = rest.astype(jnp.bfloat16)
    lo = (rest - mid.astype(jnp.float32)).astype(jnp.bfloat16)
    return hi, mid, lo


def dot3(a, b):
    a1, a2, a3 = split3(a)
    b1, b2, b3 = split3(b)
    def d(x, y):
        return jnp.dot(x, y, preferred_element_type=jnp.float32)
    return d(a1, b1) + (d(a1, b2) + d(a2, b1)) + (d(a1, b3) + d(a3, b1) + d(a2, b2))


def chol_kernel(a_ref, r_ref, w_ref, blk_ref, *, size, valid):
    panels = size // PANEL
    r_ref[...] = jnp.zeros((valid, valid), jnp.float32)
    fill_rows = lax.broadcasted_iota(jnp.int32, (size, size), 0)
    fill_cols = lax.broadcasted_iota(jnp.int32, (size, size), 1)
    w_ref[...] = jnp.where((fill_rows == fill_cols) & (fill_rows >= valid), 1.0, 0.0).astype(jnp.float32)
    w_ref[0:valid, 0:valid] = a_ref[...]
    rows = lax.broadcasted_iota(jnp.int32, (PANEL, 2 * PANEL), 0)
    lanes = lax.broadcasted_iota(jnp.int32, (PANEL, 2 * PANEL), 1)
    eye = (rows[:, :PANEL] == lanes[:, :PANEL]).astype(jnp.float32)
    group_rows = lax.broadcasted_iota(jnp.int32, (8, 1), 0)
    row_lanes = lax.broadcasted_iota(jnp.int32, (1, 2 * PANEL), 1)
    for p in range(panels):
        c0 = p * PANEL
        c1 = c0 + PANEL
        steps = min(PANEL, valid - c0)
        blk_ref[:, :PANEL] = w_ref[c0:c1, c0:c1]
        blk_ref[:, PANEL:] = eye
        if p < UNROLLED:
            groups = [blk_ref[8 * g : 8 * g + 8, :] for g in range(PANEL // 8)]
            for j in range(steps):
                own, at = divmod(j, 8)
                row = groups[own][at : at + 1, :]
                scale = lax.rsqrt(row[:, j : j + 1])
                scaled = row * scale
                for g in range(own, PANEL // 8):
                    column = groups[g][:, j : j + 1]
                    if g == own:
                        coef = jnp.where(group_rows > at, column * scale, 0.0)
                        updated = groups[g] - coef * scaled
                        groups[g] = jnp.where(group_rows == at, scaled, updated)
                    else:
                        groups[g] = groups[g] - (column * scale) * scaled
            for g in range(PANEL // 8):
                blk_ref[8 * g : 8 * g + 8, :] = groups[g]
        else:
            for first in range(0, steps, 16):
                top = (first // 8) * 8
                height = PANEL - top
                seg_rows = lax.broadcasted_iota(jnp.int32, (height, 1), 0) + top
                seg_lanes = lax.broadcasted_iota(jnp.int32, (height, PANEL), 1)

                def step(j, carry, top=top, seg_rows=seg_rows, seg_lanes=seg_lanes):
                    row = blk_ref[pl.ds(j, 1), :]
                    pivot = jnp.sum(jnp.where(row_lanes[:, :PANEL] == j, row[:, :PANEL], 0.0), axis=1, keepdims=True)
                    scale = lax.rsqrt(pivot)
                    scaled = row * scale
                    block = blk_ref[top:, :]
                    column = jnp.sum(jnp.where(seg_lanes == j, block[:, :PANEL], 0.0), axis=1, keepdims=True)
                    coef = jnp.where(seg_rows > j, column * scale, 0.0)
                    blk_ref[top:, :] = block - coef * scaled
                    blk_ref[pl.ds(j, 1), :] = scaled
                    return carry

                lax.fori_loop(first, min(first + 16, steps), step, 0)
        block = blk_ref[...]
        upper = jnp.where(lanes[:, :PANEL] >= rows[:, :PANEL], block[:, :PANEL], 0.0)
        end = min(c1, valid)
        r_ref[c0:end, c0:end] = upper[: end - c0, : end - c0]
        if p + 1 < panels:
            inv_t = block[:, PANEL:]
            right = dot3(inv_t, w_ref[c0:c1, c1:size])
            r_ref[c0:c1, c1:valid] = right[:, : valid - c1]
            w_ref[c1:size, c1:size] = w_ref[c1:size, c1:size] - dot3(right.T, right)


def cholesky_upper(gram):
    n = gram.shape[0]
    size = -(-n // PANEL) * PANEL
    return pl.pallas_call(
        functools.partial(chol_kernel, size=size, valid=n),
        out_shape=jax.ShapeDtypeStruct((n, n), jnp.float32),
        scratch_shapes=[pltpu.VMEM((size, size), jnp.float32), pltpu.VMEM((PANEL, 2 * PANEL), jnp.float32)],
    )(gram)


def neighbour_planes(block, axis, dim):
    count = lax.axis_size(axis)
    forward = [(i, i + 1) for i in range(count - 1)]
    backward = [(target, source) for source, target in forward]
    width = block.shape[dim]
    low = lax.ppermute(lax.slice_in_dim(block, width - 1, width, axis=dim), axis, forward)
    high = lax.ppermute(lax.slice_in_dim(block, 0, 1, axis=dim), axis, backward)
    return low, high


def interior_adjoint(basis, kappa):
    wide = basis.astype(jnp.float32)
    scaled = kappa[None] * wide
    padded = jnp.pad(scaled, ((0, 0), (0, 0), (1, 1), (1, 1), (1, 1)))
    center = padded[:, :, 1:-1, 1:-1, 1:-1]
    beside = padded[:, :, 2:, 1:-1, 1:-1] + padded[:, :, :-2, 1:-1, 1:-1]
    beside = beside + padded[:, :, 1:-1, 2:, 1:-1] + padded[:, :, 1:-1, :-2, 1:-1]
    beside = beside + padded[:, :, 1:-1, 1:-1, 2:] + padded[:, :, 1:-1, 1:-1, :-2]
    return wide + (beside - 6.0 * center), scaled


def butterfly_sum(x, axis):
    count = lax.axis_size(axis)
    if count & (count - 1):
        return lax.psum(x, axis)
    step = 1
    while step < count:
        x = x + lax.ppermute(x, axis, [(i, i ^ step) for i in range(count)])
        step *= 2
    return x


def butterfly_gather(x, axis, dim):
    count = lax.axis_size(axis)
    if count & (count - 1):
        return lax.all_gather(x, axis, axis=dim, tiled=True)
    index = lax.axis_index(axis)
    step = 1
    while step < count:
        other = lax.ppermute(x, axis, [(i, i ^ step) for i in range(count)])
        low = (index // step) % 2 == 0
        x = jnp.where(low, jnp.concatenate([x, other], dim), jnp.concatenate([other, x], dim))
        step *= 2
    return x


def expand_rows(coeffs_t):
    count = coeffs_t.shape[0]
    first, second = np.triu_indices(count)
    outer = (coeffs_t[:, None, :] * coeffs_t[None, :, :]).reshape(count * count, coeffs_t.shape[1])
    quad = jnp.take(outer, first * count + second, axis=0)
    ones = jnp.ones((1, coeffs_t.shape[1]), coeffs_t.dtype)
    return jnp.concatenate([ones, coeffs_t, quad], axis=0)


def project(left, right):
    return lax.dot_general(
        left,
        right,
        (((1,), (1,)), ((), ())),
        precision=lax.Precision.HIGHEST,
        preferred_element_type=jnp.float32,
    )


def body(snapshots, picks, basis, kappa):
    modes = basis.shape[0]
    stored = snapshots.shape[0]
    inner, scaled = interior_adjoint(basis, kappa)
    low, high = neighbour_planes(scaled, "space", 2)
    flat = snapshots.reshape(stored, -1).astype(jnp.float32)
    partial_t = project(inner.reshape(modes, -1), flat)
    first = snapshots[:, :, 0].reshape(stored, -1).astype(jnp.float32)
    last = snapshots[:, :, -1].reshape(stored, -1).astype(jnp.float32)
    edges = project(low.reshape(modes, -1), first) + project(high.reshape(modes, -1), last)
    partial_t = partial_t + edges
    part_t = jnp.take(partial_t, picks, axis=1)
    own_t = butterfly_sum(part_t, "space")
    coeffs_t = butterfly_gather(own_t, "tm", 1)
    features_t = expand_rows(coeffs_t)
    gram = lax.dot_general(
        features_t,
        features_t,
        (((1,), (1,)), ((), ())),
        precision=lax.Precision.HIGHEST,
        preferred_element_type=jnp.float32,
    ) / coeffs_t.shape[1]
    factor = cholesky_upper(gram)
    return (own_t.T, factor)


def solution(mesh):
    in_specs = (
        P("tm", None, "space", None, None),
        P("tm"),
        P(None, None, "space", None, None),
        P(None, "space", None, None),
    )
    out_specs = (P("tm", None), P())
    return jax.shard_map(body, mesh=mesh, in_specs=in_specs, out_specs=out_specs, check_vma=False)
```

```python
import functools

import jax
import jax.numpy as jnp
import numpy as np
from jax import lax
from jax.experimental import pallas as pl
from jax.experimental.pallas import tpu as pltpu
from jax.sharding import PartitionSpec as P

PANEL = 128
UNROLLED = 2


def split3(x):
    hi = x.astype(jnp.bfloat16)
    rest = x - hi.astype(jnp.float32)
    mid = rest.astype(jnp.bfloat16)
    lo = (rest - mid.astype(jnp.float32)).astype(jnp.bfloat16)
    return hi, mid, lo


def dot3(a, b):
    a1, a2, a3 = split3(a)
    b1, b2, b3 = split3(b)
    def d(x, y):
        return jnp.dot(x, y, preferred_element_type=jnp.float32)
    return d(a1, b1) + (d(a1, b2) + d(a2, b1)) + (d(a1, b3) + d(a3, b1) + d(a2, b2))


def chol_kernel(a_ref, r_ref, w_ref, blk_ref, *, size, valid):
    panels = size // PANEL
    r_ref[...] = jnp.zeros((valid, valid), jnp.float32)
    fill_rows = lax.broadcasted_iota(jnp.int32, (size, size), 0)
    fill_cols = lax.broadcasted_iota(jnp.int32, (size, size), 1)
    w_ref[...] = jnp.where((fill_rows == fill_cols) & (fill_rows >= valid), 1.0, 0.0).astype(jnp.float32)
    w_ref[0:valid, 0:valid] = a_ref[...]
    rows = lax.broadcasted_iota(jnp.int32, (PANEL, 2 * PANEL), 0)
    lanes = lax.broadcasted_iota(jnp.int32, (PANEL, 2 * PANEL), 1)
    eye = (rows[:, :PANEL] == lanes[:, :PANEL]).astype(jnp.float32)
    group_rows = lax.broadcasted_iota(jnp.int32, (8, 1), 0)
    row_lanes = lax.broadcasted_iota(jnp.int32, (1, 2 * PANEL), 1)
    for p in range(panels):
        c0 = p * PANEL
        c1 = c0 + PANEL
        steps = min(PANEL, valid - c0)
        blk_ref[:, :PANEL] = w_ref[c0:c1, c0:c1]
        blk_ref[:, PANEL:] = eye
        if p < UNROLLED:
            groups = [blk_ref[8 * g : 8 * g + 8, :] for g in range(PANEL // 8)]
            for j in range(steps):
                own, at = divmod(j, 8)
                row = groups[own][at : at + 1, :]
                scale = lax.rsqrt(row[:, j : j + 1])
                scaled = row * scale
                for g in range(own, PANEL // 8):
                    column = groups[g][:, j : j + 1]
                    if g == own:
                        coef = jnp.where(group_rows > at, column * scale, 0.0)
                        updated = groups[g] - coef * scaled
                        groups[g] = jnp.where(group_rows == at, scaled, updated)
                    else:
                        groups[g] = groups[g] - (column * scale) * scaled
            for g in range(PANEL // 8):
                blk_ref[8 * g : 8 * g + 8, :] = groups[g]
        else:
            for first in range(0, steps, 8):
                top = (first // 8) * 8
                height = PANEL - top
                seg_rows = lax.broadcasted_iota(jnp.int32, (height, 1), 0) + top
                seg_lanes = lax.broadcasted_iota(jnp.int32, (height, PANEL), 1)

                def step(j, carry, top=top, seg_rows=seg_rows, seg_lanes=seg_lanes):
                    row = blk_ref[pl.ds(j, 1), :]
                    pivot = jnp.sum(jnp.where(row_lanes[:, :PANEL] == j, row[:, :PANEL], 0.0), axis=1, keepdims=True)
                    scale = lax.rsqrt(pivot)
                    scaled = row * scale
                    block = blk_ref[top:, :]
                    column = jnp.sum(jnp.where(seg_lanes == j, block[:, :PANEL], 0.0), axis=1, keepdims=True)
                    coef = jnp.where(seg_rows > j, column * scale, 0.0)
                    blk_ref[top:, :] = block - coef * scaled
                    blk_ref[pl.ds(j, 1), :] = scaled
                    return carry

                lax.fori_loop(first, min(first + 8, steps), step, 0)
        block = blk_ref[...]
        upper = jnp.where(lanes[:, :PANEL] >= rows[:, :PANEL], block[:, :PANEL], 0.0)
        end = min(c1, valid)
        r_ref[c0:end, c0:end] = upper[: end - c0, : end - c0]
        if p + 1 < panels:
            inv_t = block[:, PANEL:]
            right = dot3(inv_t, w_ref[c0:c1, c1:size])
            r_ref[c0:c1, c1:valid] = right[:, : valid - c1]
            w_ref[c1:size, c1:size] = w_ref[c1:size, c1:size] - dot3(right.T, right)


def cholesky_upper(gram):
    n = gram.shape[0]
    size = -(-n // PANEL) * PANEL
    return pl.pallas_call(
        functools.partial(chol_kernel, size=size, valid=n),
        out_shape=jax.ShapeDtypeStruct((n, n), jnp.float32),
        scratch_shapes=[pltpu.VMEM((size, size), jnp.float32), pltpu.VMEM((PANEL, 2 * PANEL), jnp.float32)],
    )(gram)


def neighbour_planes(block, axis, dim):
    count = lax.axis_size(axis)
    forward = [(i, i + 1) for i in range(count - 1)]
    backward = [(target, source) for source, target in forward]
    width = block.shape[dim]
    low = lax.ppermute(lax.slice_in_dim(block, width - 1, width, axis=dim), axis, forward)
    high = lax.ppermute(lax.slice_in_dim(block, 0, 1, axis=dim), axis, backward)
    return low, high


def interior_adjoint(basis, kappa):
    wide = basis.astype(jnp.float32)
    scaled = kappa[None] * wide
    padded = jnp.pad(scaled, ((0, 0), (0, 0), (1, 1), (1, 1), (1, 1)))
    center = padded[:, :, 1:-1, 1:-1, 1:-1]
    beside = padded[:, :, 2:, 1:-1, 1:-1] + padded[:, :, :-2, 1:-1, 1:-1]
    beside = beside + padded[:, :, 1:-1, 2:, 1:-1] + padded[:, :, 1:-1, :-2, 1:-1]
    beside = beside + padded[:, :, 1:-1, 1:-1, 2:] + padded[:, :, 1:-1, 1:-1, :-2]
    return wide + (beside - 6.0 * center), scaled


def butterfly_sum(x, axis):
    count = lax.axis_size(axis)
    if count & (count - 1):
        return lax.psum(x, axis)
    step = 1
    while step < count:
        x = x + lax.ppermute(x, axis, [(i, i ^ step) for i in range(count)])
        step *= 2
    return x


def butterfly_gather(x, axis, dim):
    count = lax.axis_size(axis)
    if count & (count - 1):
        return lax.all_gather(x, axis, axis=dim, tiled=True)
    index = lax.axis_index(axis)
    step = 1
    while step < count:
        other = lax.ppermute(x, axis, [(i, i ^ step) for i in range(count)])
        low = (index // step) % 2 == 0
        x = jnp.where(low, jnp.concatenate([x, other], dim), jnp.concatenate([other, x], dim))
        step *= 2
    return x


def expand_rows(coeffs_t):
    count = coeffs_t.shape[0]
    first, second = np.triu_indices(count)
    quad = jnp.take(coeffs_t, first, axis=0) * jnp.take(coeffs_t, second, axis=0)
    ones = jnp.ones((1, coeffs_t.shape[1]), coeffs_t.dtype)
    return jnp.concatenate([ones, coeffs_t, quad], axis=0)


def project(left, right):
    return lax.dot_general(
        left,
        right,
        (((1,), (1,)), ((), ())),
        precision=lax.Precision.HIGHEST,
        preferred_element_type=jnp.float32,
    )


def body(snapshots, picks, basis, kappa):
    modes = basis.shape[0]
    stored = snapshots.shape[0]
    inner, scaled = interior_adjoint(basis, kappa)
    low, high = neighbour_planes(scaled, "space", 2)
    flat = snapshots.reshape(stored, -1).astype(jnp.float32)
    partial_t = project(inner.reshape(modes, -1), flat)
    first = snapshots[:, :, 0].reshape(stored, -1).astype(jnp.float32)
    last = snapshots[:, :, -1].reshape(stored, -1).astype(jnp.float32)
    edges = project(low.reshape(modes, -1), first) + project(high.reshape(modes, -1), last)
    partial_t = partial_t + edges
    part_t = jnp.take(partial_t, picks, axis=1)
    own_t = butterfly_sum(part_t, "space")
    coeffs_t = butterfly_gather(own_t, "tm", 1)
    features_t = expand_rows(coeffs_t)
    gram = lax.dot_general(
        features_t,
        features_t,
        (((1,), (1,)), ((), ())),
        precision=lax.Precision.HIGHEST,
        preferred_element_type=jnp.float32,
    ) / coeffs_t.shape[1]
    factor = cholesky_upper(gram)
    return (own_t.T, factor)


def solution(mesh):
    in_specs = (
        P("tm", None, "space", None, None),
        P("tm"),
        P(None, None, "space", None, None),
        P(None, "space", None, None),
    )
    out_specs = (P("tm", None), P())
    return jax.shard_map(body, mesh=mesh, in_specs=in_specs, out_specs=out_specs, check_vma=False)
```
